32 devices in a mesh: px: 4 (over z), py: 8 (over y, x, core).
Axes of the slice: x: 2, y: 2, z: 4, core: 2. Of those that a mesh axis runs over, the one named last changes fastest.
Arguments:
- right_side: float32 [8, 2048, 2048], P(None, 'py', 'px'), may hold values from -6 to 6
- solution_in: float32 [8, 2048, 2048], P(None, 'py', 'px'), may hold values from -4 to 4
- classes: int32 [8, 2048, 2048], P(None, 'py', 'px'), may hold values from 0 to 15
- coeff_table: float32 [16], replicated, may hold values from 0.2 to 5
- eigenvectors: bfloat16 [2048, 2048], replicated, may hold values from -0.053880558 to 0.053880558, as said below
- eigenvalues: float32 [2048], replicated, may hold values from 0.01 to 4
- level_shift: float32 [8], replicated, may hold values from 0.3 to 3
Outputs:
- solution: float32 [8, 2048, 2048], P(None, 'py', 'px')
- residual: float32 [8, 2048, 2048], P(None, 'py', 'px')
- direction: float32 [8, 2048, 2048], P(None, 'py', 'px')
The draws below stay inside these ranges and needn't reach their ends.
Inputs may be any that keep to these rules, and one draw needn't show every extreme that they name: eigenvectors is a symmetric matrix.
All inputs are finite; a program needn't handle non-finite values.
Results may differ from the reference program's by a relative error of at most 0.034.
Values may be sent and summed in bfloat16 or wider, within the bound.
No kernel may reach another device: no remote copies, remote signals or barrier semaphores. Data moves between devices by JAX's collectives and lax.ppermute only.
A program may use at most 128 MiB of HBM per device.

```python
import math
import jax
import jax.numpy as jnp
from jax import lax

N = 2048
NZ = 8
ITERS = 2
CLASSES = 16


def draw_eigenvectors(key, part):
    index_line = jnp.arange(N, dtype=jnp.int32) + 1
    product = index_line[:, None] * index_line[None, :] % (2 * (N + 1))
    base = math.sqrt(2.0 / (N + 1)) * jnp.sin(math.pi * product.astype(jnp.float32) / (N + 1))
    noise = jnp.clip(jax.random.normal(key, (N, N), jnp.float32), -4.0, 4.0)
    symmetric = (noise + noise.T) * (0.125 / math.sqrt(N))
    return (base + symmetric).astype(jnp.bfloat16)


def touch_ends(values, rng, smallest, top_value):
    longest = values.shape.index(max(values.shape))
    spots = []
    for shift in (0, 1):
        where = [jax.random.randint(jax.random.fold_in(rng, axis), (), 0, length) for axis, length in enumerate(values.shape)]
        where[longest] = (where[longest] + shift) % values.shape[longest]
        spots.append(tuple(where))
    return values.at[spots[0]].set(smallest).at[spots[1]].set(top_value)


def levels(own_key, extent, split, smallest, largest):
    loudness, own = 1.0, jax.random.fold_in(own_key, 6)
    for position, blocks in split:
        heights = jnp.exp(jax.random.uniform(jax.random.fold_in(own, position), (blocks,), jnp.float32, smallest / len(split), largest / len(split)))
        loudness = loudness * jnp.repeat(heights, extent[position] // blocks).reshape([-1 if axis == position else 1 for axis in range(len(extent))])
    return loudness


def scatter_about(rng, dims, scale, most, shards=(), kind=jnp.bfloat16):
    values = scale * jax.random.normal(rng, dims, jnp.float32)
    if shards:
        values = values * levels(rng, dims, shards, -0.22, 0.18)
    return jnp.clip(values, -most, most).astype(kind)


def setup_inputs(seed: int = 0) -> dict:
    seeds = jax.random.split(jax.random.key(seed), 8)
    return {
        "right_side": scatter_about(seeds[0], (NZ, N, N), 1.0, 6.0, ((1, 8), (2, 4)), jnp.float32),
        "solution_in": scatter_about(seeds[1], (NZ, N, N), 0.5, 4.0, ((1, 8), (2, 4)), jnp.float32),
        "classes": touch_ends(jax.random.randint(seeds[2], (NZ, N, N), 0, CLASSES), jax.random.fold_in(seeds[2], 1), 0, CLASSES - 1).astype(jnp.int32),
        "coeff_table": jnp.clip(jnp.exp(jax.random.uniform(seeds[3], (CLASSES,), jnp.float32, math.log(0.2), math.log(5.0))), 0.2, 5.0),
        "eigenvectors": draw_eigenvectors(jax.random.fold_in(seeds[7], 71), 0),
        "eigenvalues": jnp.clip(jnp.exp(jax.random.uniform(seeds[5], (N,), jnp.float32, math.log(0.01), math.log(4.0))), 0.01, 4.0),
        "level_shift": jnp.clip(jnp.exp(jax.random.uniform(seeds[6], (NZ,), jnp.float32, math.log(0.3), math.log(3.0))), 0.3, 3.0),
    }


def apply_operator(field, coeff):
    padded = jnp.pad(field, ((0, 0), (1, 1), (1, 1)))
    coeff_pad = jnp.pad(coeff, ((0, 0), (1, 1), (1, 1)))
    height = field.shape[1]
    width = field.shape[2]
    result = jnp.zeros_like(field)
    for shift_y, shift_x in ((0, 1), (2, 1), (1, 0), (1, 2)):
        neighbour = padded[:, shift_y:shift_y + height, shift_x:shift_x + width]
        other = coeff_pad[:, shift_y:shift_y + height, shift_x:shift_x + width]
        result = result + 0.5 * (coeff + other) * (field - neighbour)
    vertical = 0.5 * (coeff[:-1] + coeff[1:]) * (field[:-1] - field[1:])
    zero_layer = jnp.zeros_like(field[:1])
    result = result + jnp.concatenate((vertical, zero_layer), 0) - jnp.concatenate((zero_layer, vertical), 0)
    return result


def precondition(residual, eigenvectors, eigenvalues, level_shift):
    basis = eigenvectors.astype(jnp.float32)
    rounded = residual.astype(jnp.bfloat16).astype(jnp.float32)
    first = jnp.einsum('kyx,xi->kyi', rounded, basis, precision=lax.Precision.HIGHEST).astype(jnp.bfloat16)
    second = jnp.einsum('kyi,yj->kji', first.astype(jnp.float32), basis, precision=lax.Precision.HIGHEST)
    denom = eigenvalues[None, :, None] + eigenvalues[None, None, :] + level_shift[:, None, None]
    scaled = (second / denom).astype(jnp.bfloat16)
    fourth = jnp.einsum('kji,yj->kyi', scaled.astype(jnp.float32), basis, precision=lax.Precision.HIGHEST).astype(jnp.bfloat16)
    return jnp.einsum('kyi,xi->kyx', fourth.astype(jnp.float32), basis, precision=lax.Precision.HIGHEST)


def reference(right_side, solution_in, classes, coeff_table, eigenvectors, eigenvalues, level_shift):
    coeff = coeff_table[classes]
    solution = solution_in
    residual = right_side - apply_operator(solution_in, coeff)
    direction = jnp.zeros_like(residual)
    gamma_prev = jnp.float32(1.0)
    for iteration in range(ITERS):
        precond = precondition(residual, eigenvectors, eigenvalues, level_shift)
        gamma = jnp.sum(residual * precond)
        if iteration == 0:
            direction = precond
        else:
            direction = precond + (gamma / gamma_prev) * direction
        image = apply_operator(direction, coeff)
        alpha = gamma / jnp.sum(direction * image)
        solution = solution + alpha * direction
        residual = residual - alpha * image
        gamma_prev = gamma
    return solution, residual, direction
```

```python
import jax
import jax.numpy as jnp
from jax import lax
from jax.sharding import PartitionSpec as P

ITERS = 2


def padded_2(array, sides, width):
    for axis, dim in sides:
        size, length = (lax.axis_size(axis), array.shape[dim])
        up = [(i, (i + 1) % size) for i in range(size - 1)]
        down = [(j, i) for i, j in up]
        last = lax.slice_in_dim(array, length - width, length, axis=dim)
        initial = lax.slice_in_dim(array, 0, width, axis=dim)
        before = lax.ppermute(last, axis, up)
        after = lax.ppermute(initial, axis, down)
        array = jnp.concatenate([before, array, after], axis=dim)
    return array


def for_sending(array):

    def short(part):
        return part.astype(jnp.bfloat16) if part.dtype == jnp.float32 else part

    return jax.tree.map(short, array)


def all_sum(values):
    for axis in ("px", "py"):
        size = lax.axis_size(axis)
        step = 1
        while step < size:
            pairs = [(i, i ^ step) for i in range(size)]
            values = values + lax.ppermute(values, axis, pairs)
            step *= 2
    return values


def face_sum(padded, coeff_pad):
    values = padded[:, 1:-1, 1:-1]
    coeff = coeff_pad[:, 1:-1, 1:-1]
    height = values.shape[1]
    width = values.shape[2]
    result = jnp.zeros_like(values)
    for shift_y, shift_x in ((0, 1), (2, 1), (1, 0), (1, 2)):
        neighbour = padded[:, shift_y : shift_y + height, shift_x : shift_x + width]
        other = coeff_pad[:, shift_y : shift_y + height, shift_x : shift_x + width]
        result = result + 0.5 * (coeff + other) * (values - neighbour)
    vertical = 0.5 * (coeff[:-1] + coeff[1:]) * (values[:-1] - values[1:])
    zero_layer = jnp.zeros_like(values[:1])
    result = (
        result
        + jnp.concatenate((vertical, zero_layer), 0)
        - jnp.concatenate((zero_layer, vertical), 0)
    )
    return result


def precondition(residual, eigenvectors, eigenvalues, level_shift):
    rounded = residual.astype(jnp.bfloat16)
    levels_here = residual.shape[0] // lax.axis_size("px")
    first = jnp.einsum(
        "kyx,xi->kyi",
        lax.all_to_all(rounded, "px", split_axis=0, concat_axis=2, tiled=True),
        eigenvectors,
        preferred_element_type=jnp.float32,
    ).astype(jnp.bfloat16)
    second = jnp.einsum(
        "kyi,yj->kji",
        lax.all_to_all(first, "py", split_axis=2, concat_axis=1, tiled=True),
        eigenvectors,
        preferred_element_type=jnp.float32,
    )
    spectral_cols = second.shape[2]
    eigen_cols = lax.dynamic_slice_in_dim(
        eigenvalues, lax.axis_index("py") * spectral_cols, spectral_cols, 0
    )
    shift_here = lax.dynamic_slice_in_dim(
        level_shift, lax.axis_index("px") * levels_here, levels_here, 0
    )
    denom = eigenvalues[None, :, None] + eigen_cols[None, None, :] + shift_here[:, None, None]
    scaled = (second / denom).astype(jnp.bfloat16)
    fourth = jnp.einsum(
        "kji,yj->kyi", scaled, eigenvectors, preferred_element_type=jnp.float32
    ).astype(jnp.bfloat16)
    returned = lax.all_to_all(fourth, "py", split_axis=1, concat_axis=2, tiled=True)
    pencil = jnp.einsum("kyi,xi->kyx", returned, eigenvectors, preferred_element_type=jnp.float32)
    return lax.all_to_all(
        pencil.astype(jnp.bfloat16), "px", split_axis=2, concat_axis=0, tiled=True
    ).astype(pencil.dtype)


def operator(field, coeff_pad):
    padded = padded_2(for_sending(field), (("px", 2), ("py", 1)), 1).astype(field.dtype)
    return face_sum(padded, coeff_pad)


def shards(right_side, solution_in, classes, coeff_table, eigenvectors, eigenvalues, level_shift):
    coeff = jnp.zeros(classes.shape, jnp.float32)
    for label in range(coeff_table.shape[0]):
        coeff = jnp.where(classes == label, coeff_table[label], coeff)
    stacked = padded_2(
        jnp.stack((solution_in, coeff)).astype(jnp.bfloat16), (("px", 3), ("py", 2)), 1
    ).astype(jnp.float32)
    coeff_pad = stacked[1]
    solution = solution_in
    residual = right_side - face_sum(stacked[0], coeff_pad)
    direction = image = None
    gamma_prev = curvature_prev = None
    for iteration in range(ITERS):
        precond = precondition(residual, eigenvectors, eigenvalues, level_shift)
        precond_image = operator(precond, coeff_pad)
        if iteration == 0:
            sums = all_sum(jnp.stack((jnp.sum(residual * precond), jnp.sum(precond * precond_image))))
            gamma, curvature = sums[0], sums[1]
            direction, image = precond, precond_image
        else:
            sums = all_sum(
                jnp.stack(
                    (
                        jnp.sum(residual * precond),
                        jnp.sum(precond * precond_image),
                        jnp.sum(precond * image),
                        jnp.sum(direction * precond_image),
                    )
                )
            )
            gamma = sums[0]
            beta = gamma / gamma_prev
            curvature = sums[1] + beta * (sums[2] + sums[3]) + beta * beta * curvature_prev
            direction = precond + beta * direction
            image = precond_image + beta * image
        alpha = gamma / curvature
        solution = solution + alpha * direction
        residual = residual - alpha * image
        gamma_prev, curvature_prev = gamma, curvature
    return (solution, residual, direction)


def solution(mesh):
    in_specs = (P(None, "py", "px"), P(None, "py", "px"), P(None, "py", "px"), P(), P(), P(), P())
    out_specs = (P(None, "py", "px"), P(None, "py", "px"), P(None, "py", "px"))
    return jax.shard_map(shards, mesh=mesh, in_specs=in_specs, out_specs=out_specs, check_vma=False)
```

```python
import jax
import jax.numpy as jnp
from jax import lax
from jax.sharding import PartitionSpec as P

ITERS = 2


def padded_2(array, sides, width):
    for axis, dim in sides:
        size, length = (lax.axis_size(axis), array.shape[dim])
        up = [(i, (i + 1) % size) for i in range(size - 1)]
        down = [(j, i) for i, j in up]
        last = lax.slice_in_dim(array, length - width, length, axis=dim)
        initial = lax.slice_in_dim(array, 0, width, axis=dim)
        before = lax.ppermute(last, axis, up)
        after = lax.ppermute(initial, axis, down)
        array = jnp.concatenate([before, array, after], axis=dim)
    return array


def for_sending(array):

    def short(part):
        return part.astype(jnp.bfloat16) if part.dtype == jnp.float32 else part

    return jax.tree.map(short, array)


def all_sum(values):
    for axis in ("px", "py"):
        size = lax.axis_size(axis)
        step = 1
        while step < size:
            pairs = [(i, i ^ step) for i in range(size)]
            values = values + lax.ppermute(values, axis, pairs)
            step *= 2
    return values


def face_sum(padded, coeff_pad):
    values = padded[:, 1:-1, 1:-1]
    coeff = coeff_pad[:, 1:-1, 1:-1]
    height = values.shape[1]
    width = values.shape[2]
    result = jnp.zeros_like(values)
    for shift_y, shift_x in ((0, 1), (2, 1), (1, 0), (1, 2)):
        neighbour = padded[:, shift_y : shift_y + height, shift_x : shift_x + width]
        other = coeff_pad[:, shift_y : shift_y + height, shift_x : shift_x + width]
        result = result + 0.5 * (coeff + other) * (values - neighbour)
    vertical = 0.5 * (coeff[:-1] + coeff[1:]) * (values[:-1] - values[1:])
    zero_layer = jnp.zeros_like(values[:1])
    result = (
        result
        + jnp.concatenate((vertical, zero_layer), 0)
        - jnp.concatenate((zero_layer, vertical), 0)
    )
    return result


def exchange(block, axis, split_axis, concat_axis):
    size = lax.axis_size(axis)
    me = lax.axis_index(axis)
    piece = block.shape[split_axis] // size
    width = block.shape[concat_axis]
    shape = list(block.shape)
    shape[split_axis] = piece
    shape[concat_axis] = width * size
    result = jnp.zeros(shape, block.dtype)
    for shift in range(size):
        part = lax.dynamic_slice_in_dim(block, ((me + shift) % size) * piece, piece, split_axis)
        if shift:
            part = lax.ppermute(part, axis, [(i, (i + shift) % size) for i in range(size)])
        result = lax.dynamic_update_slice_in_dim(
            result, part, ((me - shift) % size) * width, concat_axis
        )
    return result


def precondition_levels(residual, first_level, eigenvectors, eigenvalues, level_shift):
    rounded = residual.astype(jnp.bfloat16)
    levels_here = residual.shape[0] // lax.axis_size("px")
    first = jnp.einsum(
        "kyx,xi->kyi",
        exchange(rounded, "px", 0, 2),
        eigenvectors,
        preferred_element_type=jnp.float32,
    ).astype(jnp.bfloat16)
    second = jnp.einsum(
        "kyi,yj->kji",
        lax.all_to_all(first, "py", split_axis=2, concat_axis=1, tiled=True),
        eigenvectors,
        preferred_element_type=jnp.float32,
    )
    spectral_cols = second.shape[2]
    eigen_cols = lax.dynamic_slice_in_dim(
        eigenvalues, lax.axis_index("py") * spectral_cols, spectral_cols, 0
    )
    shift_here = lax.dynamic_slice_in_dim(
        level_shift, first_level + lax.axis_index("px") * levels_here, levels_here, 0
    )
    denom = eigenvalues[None, :, None] + eigen_cols[None, None, :] + shift_here[:, None, None]
    scaled = (second / denom).astype(jnp.bfloat16)
    fourth = jnp.einsum(
        "kji,yj->kyi", scaled, eigenvectors, preferred_element_type=jnp.float32
    ).astype(jnp.bfloat16)
    returned = lax.all_to_all(fourth, "py", split_axis=1, concat_axis=2, tiled=True)
    pencil = jnp.einsum("kyi,xi->kyx", returned, eigenvectors, preferred_element_type=jnp.float32)
    return exchange(pencil.astype(jnp.bfloat16), "px", 2, 0).astype(pencil.dtype)


def precondition(residual, eigenvectors, eigenvalues, level_shift):
    levels = residual.shape[0]
    chunk = lax.axis_size("px")
    if levels % chunk or levels == chunk:
        chunk = levels
    parts = [
        precondition_levels(
            residual[start : start + chunk], start, eigenvectors, eigenvalues, level_shift
        )
        for start in range(0, levels, chunk)
    ]
    return jnp.concatenate(parts, 0)


def operator(field, coeff_pad):
    padded = padded_2(for_sending(field), (("px", 2), ("py", 1)), 1).astype(field.dtype)
    return face_sum(padded, coeff_pad)


def shards(right_side, solution_in, classes, coeff_table, eigenvectors, eigenvalues, level_shift):
    coeff = jnp.zeros(classes.shape, jnp.float32)
    for label in range(coeff_table.shape[0]):
        coeff = jnp.where(classes == label, coeff_table[label], coeff)
    stacked = padded_2(
        jnp.stack((solution_in, coeff)).astype(jnp.bfloat16), (("px", 3), ("py", 2)), 1
    ).astype(jnp.float32)
    coeff_pad = stacked[1]
    solution = solution_in
    residual = right_side - face_sum(stacked[0], coeff_pad)
    direction = image = None
    gamma_prev = curvature_prev = None
    for iteration in range(ITERS):
        precond = precondition(residual, eigenvectors, eigenvalues, level_shift)
        precond_image = operator(precond, coeff_pad)
        if iteration == 0:
            sums = all_sum(jnp.stack((jnp.sum(residual * precond), jnp.sum(precond * precond_image))))
            gamma, curvature = sums[0], sums[1]
            direction, image = precond, precond_image
        else:
            sums = all_sum(
                jnp.stack(
                    (
                        jnp.sum(residual * precond),
                        jnp.sum(precond * precond_image),
                        jnp.sum(precond * image),
                        jnp.sum(direction * precond_image),
                    )
                )
            )
            gamma = sums[0]
            beta = gamma / gamma_prev
            curvature = sums[1] + beta * (sums[2] + sums[3]) + beta * beta * curvature_prev
            direction = precond + beta * direction
            image = precond_image + beta * image
        alpha = gamma / curvature
        solution = solution + alpha * direction
        residual = residual - alpha * image
        gamma_prev, curvature_prev = gamma, curvature
    return (solution, residual, direction)


def solution(mesh):
    in_specs = (P(None, "py", "px"), P(None, "py", "px"), P(None, "py", "px"), P(), P(), P(), P())
    out_specs = (P(None, "py", "px"), P(None, "py", "px"), P(None, "py", "px"))
    return jax.shard_map(shards, mesh=mesh, in_specs=in_specs, out_specs=out_specs, check_vma=False)
```

```python
import jax
import jax.numpy as jnp
from jax import lax
from jax.sharding import PartitionSpec as P

ITERS = 2


def padded_2(array, sides, width):
    for axis, dim in sides:
        size, length = (lax.axis_size(axis), array.shape[dim])
        up = [(i, (i + 1) % size) for i in range(size - 1)]
        down = [(j, i) for i, j in up]
        last = lax.slice_in_dim(array, length - width, length, axis=dim)
        initial = lax.slice_in_dim(array, 0, width, axis=dim)
        before = lax.ppermute(last, axis, up)
        after = lax.ppermute(initial, axis, down)
        array = jnp.concatenate([before, array, after], axis=dim)
    return array


def for_sending(array):

    def short(part):
        return part.astype(jnp.bfloat16) if part.dtype == jnp.float32 else part

    return jax.tree.map(short, array)


def all_sum(values):
    for axis in ("px", "py"):
        size = lax.axis_size(axis)
        step = 1
        while step < size:
            pairs = [(i, i ^ step) for i in range(size)]
            values = values + lax.ppermute(values, axis, pairs)
            step *= 2
    return values


def face_sum(padded, coeff_pad):
    values = padded[:, 1:-1, 1:-1]
    coeff = coeff_pad[:, 1:-1, 1:-1]
    height = values.shape[1]
    width = values.shape[2]
    result = jnp.zeros_like(values)
    for shift_y, shift_x in ((0, 1), (2, 1), (1, 0), (1, 2)):
        neighbour = padded[:, shift_y : shift_y + height, shift_x : shift_x + width]
        other = coeff_pad[:, shift_y : shift_y + height, shift_x : shift_x + width]
        result = result + 0.5 * (coeff + other) * (values - neighbour)
    vertical = 0.5 * (coeff[:-1] + coeff[1:]) * (values[:-1] - values[1:])
    zero_layer = jnp.zeros_like(values[:1])
    result = (
        result
        + jnp.concatenate((vertical, zero_layer), 0)
        - jnp.concatenate((zero_layer, vertical), 0)
    )
    return result


def exchange(block, axis, split_axis, concat_axis):
    size = lax.axis_size(axis)
    me = lax.axis_index(axis)
    piece = block.shape[split_axis] // size
    width = block.shape[concat_axis]
    shape = list(block.shape)
    shape[split_axis] = piece
    shape[concat_axis] = width * size
    result = jnp.zeros(shape, block.dtype)
    for shift in range(size):
        part = lax.dynamic_slice_in_dim(block, ((me + shift) % size) * piece, piece, split_axis)
        if shift:
            part = lax.ppermute(part, axis, [(i, (i + shift) % size) for i in range(size)])
        result = lax.dynamic_update_slice_in_dim(
            result, part, ((me - shift) % size) * width, concat_axis
        )
    return result


def precondition_levels(residual, first_level, eigenvectors, eigenvalues, level_shift):
    across = lax.axis_size("py")
    lines = exchange(residual.astype(jnp.bfloat16), "px", 0, 2)
    levels_here, rows, width = lines.shape
    cols = width // across
    first = jnp.dot(
        lines.reshape(levels_here * rows, width), eigenvectors, preferred_element_type=jnp.float32
    ).astype(jnp.bfloat16)
    outgoing = first.reshape(levels_here * rows, across, cols).transpose(1, 0, 2)
    incoming = lax.all_to_all(outgoing, "py", 0, 0, tiled=True)
    spectral = incoming.reshape(across, levels_here, rows, cols).transpose(1, 0, 2, 3)
    spectral = spectral.reshape(levels_here, across * rows, cols)
    second = jnp.einsum("jy,kyi->kji", eigenvectors, spectral, preferred_element_type=jnp.float32)
    eigen_cols = lax.dynamic_slice_in_dim(eigenvalues, lax.axis_index("py") * cols, cols, 0)
    shift_here = lax.dynamic_slice_in_dim(
        level_shift, first_level + lax.axis_index("px") * levels_here, levels_here, 0
    )
    denom = eigenvalues[None, :, None] + eigen_cols[None, None, :] + shift_here[:, None, None]
    scaled = (second / denom).astype(jnp.bfloat16)
    fourth = jnp.einsum(
        "yj,kji->kyi", eigenvectors, scaled, preferred_element_type=jnp.float32
    ).astype(jnp.bfloat16)
    outgoing = fourth.reshape(levels_here, across, rows, cols).transpose(1, 0, 2, 3)
    returned = lax.all_to_all(outgoing, "py", 0, 0, tiled=True)
    pencil = jnp.einsum(
        "qkyi,qix->kyx",
        returned,
        eigenvectors.reshape(across, cols, width),
        preferred_element_type=jnp.float32,
    )
    return exchange(pencil.astype(jnp.bfloat16), "px", 2, 0).astype(jnp.float32)


def precondition(residual, eigenvectors, eigenvalues, level_shift):
    levels = residual.shape[0]
    chunk = lax.axis_size("px")
    if levels % chunk or levels == chunk:
        chunk = levels
    parts = [
        precondition_levels(
            residual[start : start + chunk], start, eigenvectors, eigenvalues, level_shift
        )
        for start in range(0, levels, chunk)
    ]
    return jnp.concatenate(parts, 0)


def operator(field, coeff_pad):
    padded = padded_2(for_sending(field), (("px", 2), ("py", 1)), 1).astype(field.dtype)
    return face_sum(padded, coeff_pad)


def shards(right_side, solution_in, classes, coeff_table, eigenvectors, eigenvalues, level_shift):
    coeff = jnp.zeros(classes.shape, jnp.float32)
    for label in range(coeff_table.shape[0]):
        coeff = jnp.where(classes == label, coeff_table[label], coeff)
    stacked = padded_2(
        jnp.stack((solution_in, coeff)).astype(jnp.bfloat16), (("px", 3), ("py", 2)), 1
    ).astype(jnp.float32)
    coeff_pad = stacked[1]
    solution = solution_in
    residual = right_side - face_sum(stacked[0], coeff_pad)
    direction = image = None
    gamma_prev = curvature_prev = None
    for iteration in range(ITERS):
        precond = precondition(residual, eigenvectors, eigenvalues, level_shift)
        precond_image = operator(precond, coeff_pad)
        if iteration == 0:
            sums = all_sum(jnp.stack((jnp.sum(residual * precond), jnp.sum(precond * precond_image))))
            gamma, curvature = sums[0], sums[1]
            direction, image = precond, precond_image
        else:
            sums = all_sum(
                jnp.stack(
                    (
                        jnp.sum(residual * precond),
                        jnp.sum(precond * precond_image),
                        jnp.sum(precond * image),
                        jnp.sum(direction * precond_image),
                    )
                )
            )
            gamma = sums[0]
            beta = gamma / gamma_prev
            curvature = sums[1] + beta * (sums[2] + sums[3]) + beta * beta * curvature_prev
            direction = precond + beta * direction
            image = precond_image + beta * image
        alpha = gamma / curvature
        solution = solution + alpha * direction
        residual = residual - alpha * image
        gamma_prev, curvature_prev = gamma, curvature
    return (solution, residual, direction)


def solution(mesh):
    in_specs = (P(None, "py", "px"), P(None, "py", "px"), P(None, "py", "px"), P(), P(), P(), P())
    out_specs = (P(None, "py", "px"), P(None, "py", "px"), P(None, "py", "px"))
    return jax.shard_map(shards, mesh=mesh, in_specs=in_specs, out_specs=out_specs, check_vma=False)
```

```python
import jax
import jax.numpy as jnp
from jax import lax
from jax.sharding import PartitionSpec as P

ITERS = 2


def padded_2(array, sides, width):
    for axis, dim in sides:
        size, length = (lax.axis_size(axis), array.shape[dim])
        up = [(i, (i + 1) % size) for i in range(size - 1)]
        down = [(j, i) for i, j in up]
        last = lax.slice_in_dim(array, length - width, length, axis=dim)
        initial = lax.slice_in_dim(array, 0, width, axis=dim)
        before = lax.ppermute(last, axis, up)
        after = lax.ppermute(initial, axis, down)
        array = jnp.concatenate([before, array, after], axis=dim)
    return array


def for_sending(array):

    def short(part):
        return part.astype(jnp.bfloat16) if part.dtype == jnp.float32 else part

    return jax.tree.map(short, array)


def all_sum(values):
    for axis in ("px", "py"):
        size = lax.axis_size(axis)
        step = 1
        while step < size:
            pairs = [(i, i ^ step) for i in range(size)]
            values = values + lax.ppermute(values, axis, pairs)
            step *= 2
    return values


def face_sum(padded, coeff_pad):
    values = padded[:, 1:-1, 1:-1]
    coeff = coeff_pad[:, 1:-1, 1:-1]
    height = values.shape[1]
    width = values.shape[2]
    result = jnp.zeros_like(values)
    for shift_y, shift_x in ((0, 1), (2, 1), (1, 0), (1, 2)):
        neighbour = padded[:, shift_y : shift_y + height, shift_x : shift_x + width]
        other = coeff_pad[:, shift_y : shift_y + height, shift_x : shift_x + width]
        result = result + 0.5 * (coeff + other) * (values - neighbour)
    vertical = 0.5 * (coeff[:-1] + coeff[1:]) * (values[:-1] - values[1:])
    zero_layer = jnp.zeros_like(values[:1])
    result = (
        result
        + jnp.concatenate((vertical, zero_layer), 0)
        - jnp.concatenate((zero_layer, vertical), 0)
    )
    return result


def exchange(block, axis, split_axis, concat_axis):
    size = lax.axis_size(axis)
    me = lax.axis_index(axis)
    piece = block.shape[split_axis] // size
    width = block.shape[concat_axis]
    shape = list(block.shape)
    shape[split_axis] = piece
    shape[concat_axis] = width * size
    result = jnp.zeros(shape, block.dtype)
    for shift in range(size):
        part = lax.dynamic_slice_in_dim(block, ((me + shift) % size) * piece, piece, split_axis)
        if shift:
            part = lax.ppermute(part, axis, [(i, (i + shift) % size) for i in range(size)])
        result = lax.dynamic_update_slice_in_dim(
            result, part, ((me - shift) % size) * width, concat_axis
        )
    return result


def to_lines(residual):
    return exchange(residual.astype(jnp.bfloat16), "px", 0, 2)


def transform_lines(lines, first_level, eigenvectors, eigenvalues, level_shift):
    across = lax.axis_size("py")
    levels_here, rows, width = lines.shape
    cols = width // across
    first = jnp.dot(
        lines.reshape(levels_here * rows, width), eigenvectors, preferred_element_type=jnp.float32
    ).astype(jnp.bfloat16)
    outgoing = first.reshape(levels_here * rows, across, cols).transpose(1, 0, 2)
    incoming = lax.all_to_all(outgoing, "py", 0, 0, tiled=True)
    spectral = incoming.reshape(across, levels_here, rows, cols).transpose(1, 0, 2, 3)
    spectral = spectral.reshape(levels_here, across * rows, cols)
    second = jnp.einsum("jy,kyi->kji", eigenvectors, spectral, preferred_element_type=jnp.float32)
    eigen_cols = lax.dynamic_slice_in_dim(eigenvalues, lax.axis_index("py") * cols, cols, 0)
    shift_here = lax.dynamic_slice_in_dim(
        level_shift, first_level + lax.axis_index("px") * levels_here, levels_here, 0
    )
    denom = eigenvalues[None, :, None] + eigen_cols[None, None, :] + shift_here[:, None, None]
    scaled = (second / denom).astype(jnp.bfloat16)
    fourth = jnp.einsum(
        "yj,kji->kyi", eigenvectors, scaled, preferred_element_type=jnp.float32
    ).astype(jnp.bfloat16)
    outgoing = fourth.reshape(levels_here, across, rows, cols).transpose(1, 0, 2, 3)
    returned = lax.all_to_all(outgoing, "py", 0, 0, tiled=True)
    pencil = jnp.einsum(
        "qkyi,qix->kyx",
        returned,
        eigenvectors.reshape(across, cols, width),
        preferred_element_type=jnp.float32,
    )
    return pencil.astype(jnp.bfloat16)


def precondition(residual, eigenvectors, eigenvalues, level_shift):
    levels = residual.shape[0]
    chunk = lax.axis_size("px")
    if levels % chunk or levels == chunk:
        chunk = levels
    starts = list(range(0, levels, chunk))
    lines = [to_lines(residual[start : start + chunk]) for start in starts]
    parts = []
    for index, start in enumerate(starts):
        pencil = transform_lines(lines[index], start, eigenvectors, eigenvalues, level_shift)
        if index + 1 < len(starts):
            pencil, lines[index + 1] = lax.optimization_barrier((pencil, lines[index + 1]))
        parts.append(exchange(pencil, "px", 2, 0))
    return jnp.concatenate(parts, 0).astype(jnp.float32)


def operator(field, coeff_pad):
    padded = padded_2(for_sending(field), (("px", 2), ("py", 1)), 1).astype(field.dtype)
    return face_sum(padded, coeff_pad)


def shards(right_side, solution_in, classes, coeff_table, eigenvectors, eigenvalues, level_shift):
    coeff = jnp.zeros(classes.shape, jnp.float32)
    for label in range(coeff_table.shape[0]):
        coeff = jnp.where(classes == label, coeff_table[label], coeff)
    stacked = padded_2(
        jnp.stack((solution_in, coeff)).astype(jnp.bfloat16), (("px", 3), ("py", 2)), 1
    ).astype(jnp.float32)
    coeff_pad = stacked[1]
    solution = solution_in
    residual = right_side - face_sum(stacked[0], coeff_pad)
    direction = image = None
    gamma_prev = curvature_prev = None
    for iteration in range(ITERS):
        precond = precondition(residual, eigenvectors, eigenvalues, level_shift)
        precond_image = operator(precond, coeff_pad)
        if iteration == 0:
            sums = all_sum(jnp.stack((jnp.sum(residual * precond), jnp.sum(precond * precond_image))))
            gamma, curvature = sums[0], sums[1]
            direction, image = precond, precond_image
        else:
            sums = all_sum(
                jnp.stack(
                    (
                        jnp.sum(residual * precond),
                        jnp.sum(precond * precond_image),
                        jnp.sum(precond * image),
                        jnp.sum(direction * precond_image),
                    )
                )
            )
            gamma = sums[0]
            beta = gamma / gamma_prev
            curvature = sums[1] + beta * (sums[2] + sums[3]) + beta * beta * curvature_prev
            direction = precond + beta * direction
            image = precond_image + beta * image
        alpha = gamma / curvature
        solution = solution + alpha * direction
        residual = residual - alpha * image
        gamma_prev, curvature_prev = gamma, curvature
    return (solution, residual, direction)


def solution(mesh):
    in_specs = (P(None, "py", "px"), P(None, "py", "px"), P(None, "py", "px"), P(), P(), P(), P())
    out_specs = (P(None, "py", "px"), P(None, "py", "px"), P(None, "py", "px"))
    return jax.shard_map(shards, mesh=mesh, in_specs=in_specs, out_specs=out_specs, check_vma=False)
```

```python
import jax
import jax.numpy as jnp
from jax import lax
from jax.sharding import PartitionSpec as P

ITERS = 2


def halos(array):
    slabs = []
    for axis, dim in (("py", array.ndim - 2), ("px", array.ndim - 1)):
        size, length = (lax.axis_size(axis), array.shape[dim])
        up = [(i, i + 1) for i in range(size - 1)]
        down = [(j, i) for i, j in up]
        last = lax.slice_in_dim(array, length - 1, length, axis=dim)
        initial = lax.slice_in_dim(array, 0, 1, axis=dim)
        slabs.append(lax.ppermute(last, axis, up))
        slabs.append(lax.ppermute(initial, axis, down))
    return slabs


def for_sending(array):

    def short(part):
        return part.astype(jnp.bfloat16) if part.dtype == jnp.float32 else part

    return jax.tree.map(short, array)


def all_sum(values):
    for axis in ("px", "py"):
        size = lax.axis_size(axis)
        step = 1
        while step < size:
            pairs = [(i, i ^ step) for i in range(size)]
            values = values + lax.ppermute(values, axis, pairs)
            step *= 2
    return values


def face_sum(values, coeff, value_slabs, coeff_slabs):
    def neighbours(array, slabs):
        before_y, after_y, before_x, after_x = slabs
        return (
            jnp.concatenate([before_y, array[:, :-1]], 1),
            jnp.concatenate([array[:, 1:], after_y], 1),
            jnp.concatenate([before_x, array[:, :, :-1]], 2),
            jnp.concatenate([array[:, :, 1:], after_x], 2),
        )

    result = jnp.zeros_like(values)
    for neighbour, other in zip(neighbours(values, value_slabs), neighbours(coeff, coeff_slabs)):
        result = result + 0.5 * (coeff + other) * (values - neighbour)
    vertical = 0.5 * (coeff[:-1] + coeff[1:]) * (values[:-1] - values[1:])
    zero_layer = jnp.zeros_like(values[:1])
    result = (
        result
        + jnp.concatenate((vertical, zero_layer), 0)
        - jnp.concatenate((zero_layer, vertical), 0)
    )
    return result


def exchange(block, axis, split_axis, concat_axis):
    size = lax.axis_size(axis)
    me = lax.axis_index(axis)
    piece = block.shape[split_axis] // size
    width = block.shape[concat_axis]
    shape = list(block.shape)
    shape[split_axis] = piece
    shape[concat_axis] = width * size
    result = jnp.zeros(shape, block.dtype)
    for shift in range(size):
        part = lax.dynamic_slice_in_dim(block, ((me + shift) % size) * piece, piece, split_axis)
        if shift:
            part = lax.ppermute(part, axis, [(i, (i + shift) % size) for i in range(size)])
        result = lax.dynamic_update_slice_in_dim(
            result, part, ((me - shift) % size) * width, concat_axis
        )
    return result


def precondition_levels(residual, first_level, eigenvectors, eigenvalues, level_shift):
    across = lax.axis_size("py")
    lines = exchange(residual.astype(jnp.bfloat16), "px", 0, 2)
    levels_here, rows, width = lines.shape
    cols = width // across
    first = jnp.dot(
        lines.reshape(levels_here * rows, width), eigenvectors, preferred_element_type=jnp.float32
    ).astype(jnp.bfloat16)
    outgoing = first.reshape(levels_here * rows, across, cols).transpose(1, 0, 2)
    incoming = lax.all_to_all(outgoing, "py", 0, 0, tiled=True)
    spectral = incoming.reshape(across, levels_here, rows, cols).transpose(1, 0, 2, 3)
    spectral = spectral.reshape(levels_here, across * rows, cols)
    second = jnp.einsum("jy,kyi->kji", eigenvectors, spectral, preferred_element_type=jnp.float32)
    eigen_cols = lax.dynamic_slice_in_dim(eigenvalues, lax.axis_index("py") * cols, cols, 0)
    shift_here = lax.dynamic_slice_in_dim(
        level_shift, first_level + lax.axis_index("px") * levels_here, levels_here, 0
    )
    denom = eigenvalues[None, :, None] + eigen_cols[None, None, :] + shift_here[:, None, None]
    scaled = (second / denom).astype(jnp.bfloat16)
    fourth = jnp.einsum(
        "yj,kji->kyi", eigenvectors, scaled, preferred_element_type=jnp.float32
    ).astype(jnp.bfloat16)
    outgoing = fourth.reshape(levels_here, across, rows, cols).transpose(1, 0, 2, 3)
    returned = lax.all_to_all(outgoing, "py", 0, 0, tiled=True)
    pencil = jnp.einsum(
        "qkyi,qix->kyx",
        returned,
        eigenvectors.reshape(across, cols, width),
        preferred_element_type=jnp.float32,
    )
    return exchange(pencil.astype(jnp.bfloat16), "px", 2, 0).astype(jnp.float32)


def precondition(residual, eigenvectors, eigenvalues, level_shift):
    levels = residual.shape[0]
    chunk = lax.axis_size("px")
    if levels % chunk or levels == chunk:
        chunk = levels
    parts = [
        precondition_levels(
            residual[start : start + chunk], start, eigenvectors, eigenvalues, level_shift
        )
        for start in range(0, levels, chunk)
    ]
    return jnp.concatenate(parts, 0)


def operator(field, coeff, coeff_slabs):
    slabs = [slab.astype(field.dtype) for slab in halos(for_sending(field))]
    return face_sum(field, coeff, slabs, coeff_slabs)


def shards(right_side, solution_in, classes, coeff_table, eigenvectors, eigenvalues, level_shift):
    coeff = jnp.zeros(classes.shape, jnp.float32)
    for label in range(coeff_table.shape[0]):
        coeff = jnp.where(classes == label, coeff_table[label], coeff)
    stacked = halos(jnp.stack((solution_in, coeff)).astype(jnp.bfloat16))
    solution_slabs = [slab[0].astype(jnp.float32) for slab in stacked]
    coeff_slabs = [slab[1].astype(jnp.float32) for slab in stacked]
    solution = solution_in
    residual = right_side - face_sum(solution_in, coeff, solution_slabs, coeff_slabs)
    direction = image = None
    gamma_prev = curvature_prev = None
    for iteration in range(ITERS):
        precond = precondition(residual, eigenvectors, eigenvalues, level_shift)
        precond_image = operator(precond, coeff, coeff_slabs)
        if iteration == 0:
            sums = all_sum(jnp.stack((jnp.sum(residual * precond), jnp.sum(precond * precond_image))))
            gamma, curvature = sums[0], sums[1]
            direction, image = precond, precond_image
        else:
            sums = all_sum(
                jnp.stack(
                    (
                        jnp.sum(residual * precond),
                        jnp.sum(precond * precond_image),
                        jnp.sum(precond * image),
                        jnp.sum(direction * precond_image),
                    )
                )
            )
            gamma = sums[0]
            beta = gamma / gamma_prev
            curvature = sums[1] + beta * (sums[2] + sums[3]) + beta * beta * curvature_prev
            direction = precond + beta * direction
            image = precond_image + beta * image
        alpha = gamma / curvature
        solution = solution + alpha * direction
        residual = residual - alpha * image
        gamma_prev, curvature_prev = gamma, curvature
    return (solution, residual, direction)


def solution(mesh):
    in_specs = (P(None, "py", "px"), P(None, "py", "px"), P(None, "py", "px"), P(), P(), P(), P())
    out_specs = (P(None, "py", "px"), P(None, "py", "px"), P(None, "py", "px"))
    return jax.shard_map(shards, mesh=mesh, in_specs=in_specs, out_specs=out_specs, check_vma=False)
```

```python
import jax
import jax.numpy as jnp
from jax import lax
from jax.sharding import PartitionSpec as P

ITERS = 2


def padded_2(array, sides, width):
    slabs = {}
    for axis, dim in sides:
        size, length = (lax.axis_size(axis), array.shape[dim])
        up = [(i, (i + 1) % size) for i in range(size - 1)]
        down = [(j, i) for i, j in up]
        last = lax.slice_in_dim(array, length - width, length, axis=dim)
        initial = lax.slice_in_dim(array, 0, width, axis=dim)
        slabs[dim] = (lax.ppermute(last, axis, up), lax.ppermute(initial, axis, down))
    for position, (axis, dim) in enumerate(sides):
        before, after = slabs[dim]
        for _, other in sides[:position]:
            pad = [(0, 0)] * array.ndim
            pad[other] = (width, width)
            before = jnp.pad(before, pad)
            after = jnp.pad(after, pad)
        array = jnp.concatenate([before, array, after], axis=dim)
    return array


def for_sending(array):

    def short(part):
        return part.astype(jnp.bfloat16) if part.dtype == jnp.float32 else part

    return jax.tree.map(short, array)


def all_sum(values):
    for axis in ("px", "py"):
        size = lax.axis_size(axis)
        step = 1
        while step < size:
            pairs = [(i, i ^ step) for i in range(size)]
            values = values + lax.ppermute(values, axis, pairs)
            step *= 2
    return values


def face_sum(padded, coeff_pad):
    values = padded[:, 1:-1, 1:-1]
    coeff = coeff_pad[:, 1:-1, 1:-1]
    height = values.shape[1]
    width = values.shape[2]
    result = jnp.zeros_like(values)
    for shift_y, shift_x in ((0, 1), (2, 1), (1, 0), (1, 2)):
        neighbour = padded[:, shift_y : shift_y + height, shift_x : shift_x + width]
        other = coeff_pad[:, shift_y : shift_y + height, shift_x : shift_x + width]
        result = result + 0.5 * (coeff + other) * (values - neighbour)
    vertical = 0.5 * (coeff[:-1] + coeff[1:]) * (values[:-1] - values[1:])
    zero_layer = jnp.zeros_like(values[:1])
    result = (
        result
        + jnp.concatenate((vertical, zero_layer), 0)
        - jnp.concatenate((zero_layer, vertical), 0)
    )
    return result


def exchange(block, axis, split_axis, concat_axis):
    size = lax.axis_size(axis)
    me = lax.axis_index(axis)
    piece = block.shape[split_axis] // size
    width = block.shape[concat_axis]
    shape = list(block.shape)
    shape[split_axis] = piece
    shape[concat_axis] = width * size
    result = jnp.zeros(shape, block.dtype)
    for shift in range(size):
        part = lax.dynamic_slice_in_dim(block, ((me + shift) % size) * piece, piece, split_axis)
        if shift:
            part = lax.ppermute(part, axis, [(i, (i + shift) % size) for i in range(size)])
        result = lax.dynamic_update_slice_in_dim(
            result, part, ((me - shift) % size) * width, concat_axis
        )
    return result


def precondition_levels(residual, first_level, eigenvectors, eigenvalues, level_shift):
    across = lax.axis_size("py")
    lines = exchange(residual.astype(jnp.bfloat16), "px", 0, 2)
    levels_here, rows, width = lines.shape
    cols = width // across
    first = jnp.dot(
        lines.reshape(levels_here * rows, width), eigenvectors, preferred_element_type=jnp.float32
    ).astype(jnp.bfloat16)
    outgoing = first.reshape(levels_here * rows, across, cols).transpose(1, 0, 2)
    incoming = lax.all_to_all(outgoing, "py", 0, 0, tiled=True)
    spectral = incoming.reshape(across, levels_here, rows, cols).transpose(1, 0, 2, 3)
    spectral = spectral.reshape(levels_here, across * rows, cols)
    second = jnp.einsum("jy,kyi->kji", eigenvectors, spectral, preferred_element_type=jnp.float32)
    eigen_cols = lax.dynamic_slice_in_dim(eigenvalues, lax.axis_index("py") * cols, cols, 0)
    shift_here = lax.dynamic_slice_in_dim(
        level_shift, first_level + lax.axis_index("px") * levels_here, levels_here, 0
    )
    denom = eigenvalues[None, :, None] + eigen_cols[None, None, :] + shift_here[:, None, None]
    scaled = (second / denom).astype(jnp.bfloat16)
    fourth = jnp.einsum(
        "yj,kji->kyi", eigenvectors, scaled, preferred_element_type=jnp.float32
    ).astype(jnp.bfloat16)
    outgoing = fourth.reshape(levels_here, across, rows, cols).transpose(1, 0, 2, 3)
    returned = lax.all_to_all(outgoing, "py", 0, 0, tiled=True)
    pencil = jnp.einsum(
        "qkyi,qix->kyx",
        returned,
        eigenvectors.reshape(across, cols, width),
        preferred_element_type=jnp.float32,
    )
    return exchange(pencil.astype(jnp.bfloat16), "px", 2, 0).astype(jnp.float32)


def precondition(residual, eigenvectors, eigenvalues, level_shift):
    levels = residual.shape[0]
    chunk = lax.axis_size("px")
    if levels % chunk or levels == chunk:
        chunk = levels
    parts = [
        precondition_levels(
            residual[start : start + chunk], start, eigenvectors, eigenvalues, level_shift
        )
        for start in range(0, levels, chunk)
    ]
    return jnp.concatenate(parts, 0)


def operator(field, coeff_pad):
    padded = padded_2(for_sending(field), (("px", 2), ("py", 1)), 1).astype(field.dtype)
    return face_sum(padded, coeff_pad)


def shards(right_side, solution_in, classes, coeff_table, eigenvectors, eigenvalues, level_shift):
    coeff = jnp.zeros(classes.shape, jnp.float32)
    for label in range(coeff_table.shape[0]):
        coeff = jnp.where(classes == label, coeff_table[label], coeff)
    stacked = padded_2(
        jnp.stack((solution_in, coeff)).astype(jnp.bfloat16), (("px", 3), ("py", 2)), 1
    ).astype(jnp.float32)
    coeff_pad = stacked[1]
    solution = solution_in
    residual = right_side - face_sum(stacked[0], coeff_pad)
    direction = image = None
    gamma_prev = curvature_prev = None
    for iteration in range(ITERS):
        precond = precondition(residual, eigenvectors, eigenvalues, level_shift)
        precond_image = operator(precond, coeff_pad)
        if iteration == 0:
            sums = all_sum(jnp.stack((jnp.sum(residual * precond), jnp.sum(precond * precond_image))))
            gamma, curvature = sums[0], sums[1]
            direction, image = precond, precond_image
        else:
            sums = all_sum(
                jnp.stack(
                    (
                        jnp.sum(residual * precond),
                        jnp.sum(precond * precond_image),
                        jnp.sum(precond * image),
                        jnp.sum(direction * precond_image),
                    )
                )
            )
            gamma = sums[0]
            beta = gamma / gamma_prev
            curvature = sums[1] + beta * (sums[2] + sums[3]) + beta * beta * curvature_prev
            direction = precond + beta * direction
            image = precond_image + beta * image
        alpha = gamma / curvature
        solution = solution + alpha * direction
        residual = residual - alpha * image
        gamma_prev, curvature_prev = gamma, curvature
    return (solution, residual, direction)


def solution(mesh):
    in_specs = (P(None, "py", "px"), P(None, "py", "px"), P(None, "py", "px"), P(), P(), P(), P())
    out_specs = (P(None, "py", "px"), P(None, "py", "px"), P(None, "py", "px"))
    return jax.shard_map(shards, mesh=mesh, in_specs=in_specs, out_specs=out_specs, check_vma=False)
```

```python
import jax
import jax.numpy as jnp
from jax import lax
from jax.sharding import PartitionSpec as P

ITERS = 2


def padded_2(array, sides, width):
    slabs = {}
    for axis, dim in sides:
        size, length = (lax.axis_size(axis), array.shape[dim])
        up = [(i, (i + 1) % size) for i in range(size - 1)]
        down = [(j, i) for i, j in up]
        last = lax.slice_in_dim(array, length - width, length, axis=dim)
        initial = lax.slice_in_dim(array, 0, width, axis=dim)
        slabs[dim] = (lax.ppermute(last, axis, up), lax.ppermute(initial, axis, down))
    for position, (axis, dim) in enumerate(sides):
        before, after = slabs[dim]
        for _, other in sides[:position]:
            pad = [(0, 0)] * array.ndim
            pad[other] = (width, width)
            before = jnp.pad(before, pad)
            after = jnp.pad(after, pad)
        array = jnp.concatenate([before, array, after], axis=dim)
    return array


def for_sending(array):

    def short(part):
        return part.astype(jnp.bfloat16) if part.dtype == jnp.float32 else part

    return jax.tree.map(short, array)


def all_sum(values):
    axes = ("px", "py")
    count = lax.axis_size(axes)
    spread = jnp.broadcast_to(values[None], (count,) + values.shape)
    return jnp.sum(lax.all_to_all(spread, axes, 0, 0, tiled=True), 0)


def face_sum(padded, coeff_pad):
    values = padded[:, 1:-1, 1:-1]
    coeff = coeff_pad[:, 1:-1, 1:-1]
    height = values.shape[1]
    width = values.shape[2]
    result = jnp.zeros_like(values)
    for shift_y, shift_x in ((0, 1), (2, 1), (1, 0), (1, 2)):
        neighbour = padded[:, shift_y : shift_y + height, shift_x : shift_x + width]
        other = coeff_pad[:, shift_y : shift_y + height, shift_x : shift_x + width]
        result = result + 0.5 * (coeff + other) * (values - neighbour)
    vertical = 0.5 * (coeff[:-1] + coeff[1:]) * (values[:-1] - values[1:])
    zero_layer = jnp.zeros_like(values[:1])
    result = (
        result
        + jnp.concatenate((vertical, zero_layer), 0)
        - jnp.concatenate((zero_layer, vertical), 0)
    )
    return result


def exchange(block, axis, split_axis, concat_axis):
    size = lax.axis_size(axis)
    me = lax.axis_index(axis)
    piece = block.shape[split_axis] // size
    width = block.shape[concat_axis]
    shape = list(block.shape)
    shape[split_axis] = piece
    shape[concat_axis] = width * size
    result = jnp.zeros(shape, block.dtype)
    for shift in range(size):
        part = lax.dynamic_slice_in_dim(block, ((me + shift) % size) * piece, piece, split_axis)
        if shift:
            part = lax.ppermute(part, axis, [(i, (i + shift) % size) for i in range(size)])
        result = lax.dynamic_update_slice_in_dim(
            result, part, ((me - shift) % size) * width, concat_axis
        )
    return result


def precondition_lines(lines, first_level, eigenvectors, eigenvalues, level_shift):
    across = lax.axis_size("py")
    levels_here, rows, width = lines.shape
    cols = width // across
    first = jnp.dot(
        lines.reshape(levels_here * rows, width), eigenvectors, preferred_element_type=jnp.float32
    ).astype(jnp.bfloat16)
    outgoing = first.reshape(levels_here * rows, across, cols).transpose(1, 0, 2)
    incoming = lax.all_to_all(outgoing, "py", 0, 0, tiled=True)
    spectral = incoming.reshape(across, levels_here, rows, cols).transpose(1, 0, 2, 3)
    spectral = spectral.reshape(levels_here, across * rows, cols)
    second = jnp.einsum("jy,kyi->kji", eigenvectors, spectral, preferred_element_type=jnp.float32)
    eigen_cols = lax.dynamic_slice_in_dim(eigenvalues, lax.axis_index("py") * cols, cols, 0)
    shift_here = lax.dynamic_slice_in_dim(
        level_shift, first_level + lax.axis_index("px") * levels_here, levels_here, 0
    )
    denom = eigenvalues[None, :, None] + eigen_cols[None, None, :] + shift_here[:, None, None]
    scaled = (second / denom).astype(jnp.bfloat16)
    fourth = jnp.einsum(
        "yj,kji->kyi", eigenvectors, scaled, preferred_element_type=jnp.float32
    ).astype(jnp.bfloat16)
    outgoing = fourth.reshape(levels_here, across, rows, cols).transpose(1, 0, 2, 3)
    returned = lax.all_to_all(outgoing, "py", 0, 0, tiled=True)
    pencil = jnp.einsum(
        "qkyi,qix->kyx",
        returned,
        eigenvectors.reshape(across, cols, width),
        preferred_element_type=jnp.float32,
    )
    return exchange(pencil.astype(jnp.bfloat16), "px", 2, 0).astype(jnp.float32)


def precondition(residual, eigenvectors, eigenvalues, level_shift):
    levels = residual.shape[0]
    chunk = lax.axis_size("px")
    if levels % chunk or levels == chunk:
        chunk = levels
    parts = []
    waiting = residual
    for start in range(0, levels, chunk):
        lines = exchange(waiting[start : start + chunk].astype(jnp.bfloat16), "px", 0, 2)
        lines, waiting = lax.optimization_barrier((lines, waiting))
        parts.append(precondition_lines(lines, start, eigenvectors, eigenvalues, level_shift))
    return jnp.concatenate(parts, 0)


def operator(field, coeff_pad):
    padded = padded_2(for_sending(field), (("px", 2), ("py", 1)), 1).astype(field.dtype)
    return face_sum(padded, coeff_pad)


def shards(right_side, solution_in, classes, coeff_table, eigenvectors, eigenvalues, level_shift):
    coeff = jnp.zeros(classes.shape, jnp.float32)
    for label in range(coeff_table.shape[0]):
        coeff = jnp.where(classes == label, coeff_table[label], coeff)
    stacked = padded_2(
        jnp.stack((solution_in, coeff)).astype(jnp.bfloat16), (("px", 3), ("py", 2)), 1
    ).astype(jnp.float32)
    coeff_pad = stacked[1]
    solution = solution_in
    residual = right_side - face_sum(stacked[0], coeff_pad)
    direction = image = None
    gamma_prev = curvature_prev = None
    for iteration in range(ITERS):
        precond = precondition(residual, eigenvectors, eigenvalues, level_shift)
        precond_image = operator(precond, coeff_pad)
        if iteration == 0:
            sums = all_sum(jnp.stack((jnp.sum(residual * precond), jnp.sum(precond * precond_image))))
            gamma, curvature = sums[0], sums[1]
            direction, image = precond, precond_image
        else:
            sums = all_sum(
                jnp.stack(
                    (
                        jnp.sum(residual * precond),
                        jnp.sum(precond * precond_image),
                        jnp.sum(precond * image),
                        jnp.sum(direction * precond_image),
                    )
                )
            )
            gamma = sums[0]
            beta = gamma / gamma_prev
            curvature = sums[1] + beta * (sums[2] + sums[3]) + beta * beta * curvature_prev
            direction = precond + beta * direction
            image = precond_image + beta * image
        alpha = gamma / curvature
        solution = solution + alpha * direction
        residual = residual - alpha * image
        gamma_prev, curvature_prev = gamma, curvature
    return (solution, residual, direction)


def solution(mesh):
    in_specs = (P(None, "py", "px"), P(None, "py", "px"), P(None, "py", "px"), P(), P(), P(), P())
    out_specs = (P(None, "py", "px"), P(None, "py", "px"), P(None, "py", "px"))
    return jax.shard_map(shards, mesh=mesh, in_specs=in_specs, out_specs=out_specs, check_vma=False)
```

```python
import jax
import jax.numpy as jnp
from jax import lax
from jax.sharding import PartitionSpec as P

ITERS = 2


def padded_2(array, sides, width):
    slabs = {}
    for axis, dim in sides:
        size, length = (lax.axis_size(axis), array.shape[dim])
        up = [(i, (i + 1) % size) for i in range(size - 1)]
        down = [(j, i) for i, j in up]
        last = lax.slice_in_dim(array, length - width, length, axis=dim)
        initial = lax.slice_in_dim(array, 0, width, axis=dim)
        slabs[dim] = (lax.ppermute(last, axis, up), lax.ppermute(initial, axis, down))
    for position, (axis, dim) in enumerate(sides):
        before, after = slabs[dim]
        for _, other in sides[:position]:
            pad = [(0, 0)] * array.ndim
            pad[other] = (width, width)
            before = jnp.pad(before, pad)
            after = jnp.pad(after, pad)
        array = jnp.concatenate([before, array, after], axis=dim)
    return array


def for_sending(array):

    def short(part):
        return part.astype(jnp.bfloat16) if part.dtype == jnp.float32 else part

    return jax.tree.map(short, array)


def all_sum(values):
    axes = ("px", "py")
    count = lax.axis_size(axes)
    spread = jnp.broadcast_to(values[None], (count,) + values.shape)
    return jnp.sum(lax.all_to_all(spread, axes, 0, 0, tiled=True), 0)


def face_sum(padded, coeff_pad):
    values = padded[:, 1:-1, 1:-1]
    coeff = coeff_pad[:, 1:-1, 1:-1]
    height = values.shape[1]
    width = values.shape[2]
    result = jnp.zeros_like(values)
    for shift_y, shift_x in ((0, 1), (2, 1), (1, 0), (1, 2)):
        neighbour = padded[:, shift_y : shift_y + height, shift_x : shift_x + width]
        other = coeff_pad[:, shift_y : shift_y + height, shift_x : shift_x + width]
        result = result + 0.5 * (coeff + other) * (values - neighbour)
    vertical = 0.5 * (coeff[:-1] + coeff[1:]) * (values[:-1] - values[1:])
    zero_layer = jnp.zeros_like(values[:1])
    result = (
        result
        + jnp.concatenate((vertical, zero_layer), 0)
        - jnp.concatenate((zero_layer, vertical), 0)
    )
    return result


def exchange(block, axis, split_axis, concat_axis):
    size = lax.axis_size(axis)
    me = lax.axis_index(axis)
    piece = block.shape[split_axis] // size
    width = block.shape[concat_axis]
    shape = list(block.shape)
    shape[split_axis] = piece
    shape[concat_axis] = width * size
    result = jnp.zeros(shape, block.dtype)
    for shift in range(size):
        part = lax.dynamic_slice_in_dim(block, ((me + shift) % size) * piece, piece, split_axis)
        if shift:
            part = lax.ppermute(part, axis, [(i, (i + shift) % size) for i in range(size)])
        result = lax.dynamic_update_slice_in_dim(
            result, part, ((me - shift) % size) * width, concat_axis
        )
    return result


def spectrum(lines, first_level, eigenvectors, eigenvalues, level_shift):
    across = lax.axis_size("py")
    levels_here, rows, width = lines.shape
    cols = width // across
    first = jnp.dot(
        lines.reshape(levels_here * rows, width), eigenvectors, preferred_element_type=jnp.float32
    ).astype(jnp.bfloat16)
    outgoing = first.reshape(levels_here * rows, across, cols).transpose(1, 0, 2)
    incoming = lax.all_to_all(outgoing, "py", 0, 0, tiled=True)
    spectral = incoming.reshape(across, levels_here, rows, cols).transpose(1, 0, 2, 3)
    spectral = spectral.reshape(levels_here, across * rows, cols)
    second = jnp.einsum("jy,kyi->kji", eigenvectors, spectral, preferred_element_type=jnp.float32)
    eigen_cols = lax.dynamic_slice_in_dim(eigenvalues, lax.axis_index("py") * cols, cols, 0)
    shift_here = lax.dynamic_slice_in_dim(
        level_shift, first_level + lax.axis_index("px") * levels_here, levels_here, 0
    )
    denom = eigenvalues[None, :, None] + eigen_cols[None, None, :] + shift_here[:, None, None]
    return (second / denom).astype(jnp.bfloat16)


def pencil_of(scaled, eigenvectors):
    across = lax.axis_size("py")
    levels_here, height, cols = scaled.shape
    rows = height // across
    width = cols * across
    fourth = jnp.einsum(
        "yj,kji->kyi", eigenvectors, scaled, preferred_element_type=jnp.float32
    ).astype(jnp.bfloat16)
    outgoing = fourth.reshape(levels_here, across, rows, cols).transpose(1, 0, 2, 3)
    returned = lax.all_to_all(outgoing, "py", 0, 0, tiled=True)
    pencil = jnp.einsum(
        "qkyi,qix->kyx",
        returned,
        eigenvectors.reshape(across, cols, width),
        preferred_element_type=jnp.float32,
    )
    return pencil.astype(jnp.bfloat16)


def precondition(residual, eigenvectors, eigenvalues, level_shift):
    levels = residual.shape[0]
    chunk = lax.axis_size("px")
    if levels % chunk or levels == chunk:
        chunk = levels
    starts = list(range(0, levels, chunk))
    spectra = []
    waiting = residual
    for start in starts:
        lines = exchange(waiting[start : start + chunk].astype(jnp.bfloat16), "px", 0, 2)
        lines, waiting = lax.optimization_barrier((lines, waiting))
        spectra.append(spectrum(lines, start, eigenvectors, eigenvalues, level_shift))
    parts = []
    for index in range(len(starts)):
        pencil = pencil_of(spectra[index], eigenvectors)
        if index + 1 < len(starts):
            pencil, spectra[index + 1] = lax.optimization_barrier((pencil, spectra[index + 1]))
        parts.append(exchange(pencil, "px", 2, 0))
    return jnp.concatenate(parts, 0).astype(jnp.float32)


def operator(field, coeff_pad):
    padded = padded_2(for_sending(field), (("px", 2), ("py", 1)), 1).astype(field.dtype)
    return face_sum(padded, coeff_pad)


def shards(right_side, solution_in, classes, coeff_table, eigenvectors, eigenvalues, level_shift):
    coeff = jnp.zeros(classes.shape, jnp.float32)
    for label in range(coeff_table.shape[0]):
        coeff = jnp.where(classes == label, coeff_table[label], coeff)
    solution_pad, coeff_pad = (
        padded_2(array.astype(jnp.bfloat16), (("px", 2), ("py", 1)), 1).astype(jnp.float32)
        for array in (solution_in, coeff)
    )
    solution = solution_in
    residual = right_side - face_sum(solution_pad, coeff_pad)
    direction = image = None
    gamma_prev = curvature_prev = None
    for iteration in range(ITERS):
        precond = precondition(residual, eigenvectors, eigenvalues, level_shift)
        precond_image = operator(precond, coeff_pad)
        if iteration == 0:
            sums = all_sum(jnp.stack((jnp.sum(residual * precond), jnp.sum(precond * precond_image))))
            gamma, curvature = sums[0], sums[1]
            direction, image = precond, precond_image
        else:
            sums = all_sum(
                jnp.stack(
                    (
                        jnp.sum(residual * precond),
                        jnp.sum(precond * precond_image),
                        jnp.sum(precond * image),
                        jnp.sum(direction * precond_image),
                    )
                )
            )
            gamma = sums[0]
            beta = gamma / gamma_prev
            curvature = sums[1] + beta * (sums[2] + sums[3]) + beta * beta * curvature_prev
            direction = precond + beta * direction
            image = precond_image + beta * image
        alpha = gamma / curvature
        solution = solution + alpha * direction
        residual = residual - alpha * image
        gamma_prev, curvature_prev = gamma, curvature
    return (solution, residual, direction)


def solution(mesh):
    in_specs = (P(None, "py", "px"), P(None, "py", "px"), P(None, "py", "px"), P(), P(), P(), P())
    out_specs = (P(None, "py", "px"), P(None, "py", "px"), P(None, "py", "px"))
    return jax.shard_map(shards, mesh=mesh, in_specs=in_specs, out_specs=out_specs, check_vma=False)
```

```python
import jax
import jax.numpy as jnp
from jax import lax
from jax.sharding import PartitionSpec as P

ITERS = 2


def padded_2(array, sides, width):
    slabs = {}
    for axis, dim in sides:
        size, length = (lax.axis_size(axis), array.shape[dim])
        up = [(i, (i + 1) % size) for i in range(size - 1)]
        down = [(j, i) for i, j in up]
        last = lax.slice_in_dim(array, length - width, length, axis=dim)
        initial = lax.slice_in_dim(array, 0, width, axis=dim)
        slabs[dim] = (lax.ppermute(last, axis, up), lax.ppermute(initial, axis, down))
    for position, (axis, dim) in enumerate(sides):
        before, after = slabs[dim]
        for _, other in sides[:position]:
            pad = [(0, 0)] * array.ndim
            pad[other] = (width, width)
            before = jnp.pad(before, pad)
            after = jnp.pad(after, pad)
        array = jnp.concatenate([before, array, after], axis=dim)
    return array


def for_sending(array):

    def short(part):
        return part.astype(jnp.bfloat16) if part.dtype == jnp.float32 else part

    return jax.tree.map(short, array)


def all_sum(values):
    axes = ("px", "py")
    count = lax.axis_size(axes)
    spread = jnp.broadcast_to(values[None], (count,) + values.shape)
    return jnp.sum(lax.all_to_all(spread, axes, 0, 0, tiled=True), 0)


def face_sum(padded, coeff_pad):
    values = padded[:, 1:-1, 1:-1]
    coeff = coeff_pad[:, 1:-1, 1:-1]
    height = values.shape[1]
    width = values.shape[2]
    result = jnp.zeros_like(values)
    for shift_y, shift_x in ((0, 1), (2, 1), (1, 0), (1, 2)):
        neighbour = padded[:, shift_y : shift_y + height, shift_x : shift_x + width]
        other = coeff_pad[:, shift_y : shift_y + height, shift_x : shift_x + width]
        result = result + 0.5 * (coeff + other) * (values - neighbour)
    coeff_next = jnp.concatenate((coeff[1:], coeff[-1:]), 0)
    values_next = jnp.concatenate((values[1:], values[-1:]), 0)
    downward = 0.5 * (coeff + coeff_next) * (values - values_next)
    upward = jnp.concatenate((jnp.zeros_like(downward[:1]), downward[:-1]), 0)
    return result + downward - upward


def exchange(block, axis, split_axis, concat_axis):
    size = lax.axis_size(axis)
    me = lax.axis_index(axis)
    piece = block.shape[split_axis] // size
    width = block.shape[concat_axis]
    shape = list(block.shape)
    shape[split_axis] = piece
    shape[concat_axis] = width * size
    result = jnp.zeros(shape, block.dtype)
    for shift in range(size):
        part = lax.dynamic_slice_in_dim(block, ((me + shift) % size) * piece, piece, split_axis)
        if shift:
            part = lax.ppermute(part, axis, [(i, (i + shift) % size) for i in range(size)])
        result = lax.dynamic_update_slice_in_dim(
            result, part, ((me - shift) % size) * width, concat_axis
        )
    return result


def precondition_lines(lines, first_level, eigenvectors, eigenvalues, level_shift):
    across = lax.axis_size("py")
    levels_here, rows, width = lines.shape
    cols = width // across
    first = jnp.dot(
        lines.reshape(levels_here * rows, width), eigenvectors, preferred_element_type=jnp.float32
    ).astype(jnp.bfloat16)
    outgoing = first.reshape(levels_here * rows, across, cols).transpose(1, 0, 2)
    incoming = lax.all_to_all(outgoing, "py", 0, 0, tiled=True)
    spectral = incoming.reshape(across, levels_here, rows, cols).transpose(1, 0, 2, 3)
    spectral = spectral.reshape(levels_here, across * rows, cols)
    second = jnp.einsum("jy,kyi->kji", eigenvectors, spectral, preferred_element_type=jnp.float32)
    eigen_cols = lax.dynamic_slice_in_dim(eigenvalues, lax.axis_index("py") * cols, cols, 0)
    shift_here = lax.dynamic_slice_in_dim(
        level_shift, first_level + lax.axis_index("px") * levels_here, levels_here, 0
    )
    denom = eigenvalues[None, :, None] + eigen_cols[None, None, :] + shift_here[:, None, None]
    scaled = (second / denom).astype(jnp.bfloat16)
    fourth = jnp.einsum(
        "yj,kji->kyi", eigenvectors, scaled, preferred_element_type=jnp.float32
    ).astype(jnp.bfloat16)
    outgoing = fourth.reshape(levels_here, across, rows, cols).transpose(1, 0, 2, 3)
    returned = lax.all_to_all(outgoing, "py", 0, 0, tiled=True)
    pencil = jnp.einsum(
        "qkyi,qix->kyx",
        returned,
        eigenvectors.reshape(across, cols, width),
        preferred_element_type=jnp.float32,
    )
    return exchange(pencil.astype(jnp.bfloat16), "px", 2, 0).astype(jnp.float32)


def precondition(residual, eigenvectors, eigenvalues, level_shift):
    levels = residual.shape[0]
    chunk = lax.axis_size("px")
    if levels % chunk or levels == chunk:
        chunk = levels
    parts = []
    waiting = residual
    for start in range(0, levels, chunk):
        lines = exchange(waiting[start : start + chunk].astype(jnp.bfloat16), "px", 0, 2)
        lines, waiting = lax.optimization_barrier((lines, waiting))
        parts.append(precondition_lines(lines, start, eigenvectors, eigenvalues, level_shift))
    return jnp.concatenate(parts, 0)


def operator(field, coeff_pad):
    padded = padded_2(for_sending(field), (("px", 2), ("py", 1)), 1).astype(field.dtype)
    return face_sum(padded, coeff_pad)


def shards(right_side, solution_in, classes, coeff_table, eigenvectors, eigenvalues, level_shift):
    labels = classes.astype(jnp.bfloat16)
    table = coeff_table.astype(jnp.bfloat16)
    coeff = jnp.zeros(classes.shape, jnp.bfloat16)
    for label in range(coeff_table.shape[0]):
        coeff = jnp.where(labels == label, table[label], coeff)
    stacked = padded_2(
        jnp.stack((solution_in, coeff)).astype(jnp.bfloat16), (("px", 3), ("py", 2)), 1
    ).astype(jnp.float32)
    coeff_pad = stacked[1]
    solution = solution_in
    residual = right_side - face_sum(stacked[0], coeff_pad)
    direction = image = None
    gamma_prev = curvature_prev = None
    for iteration in range(ITERS):
        precond = precondition(residual, eigenvectors, eigenvalues, level_shift)
        precond_image = operator(precond, coeff_pad)
        if iteration == 0:
            sums = all_sum(jnp.stack((jnp.sum(residual * precond), jnp.sum(precond * precond_image))))
            gamma, curvature = sums[0], sums[1]
            direction, image = precond, precond_image
        else:
            sums = all_sum(
                jnp.stack(
                    (
                        jnp.sum(residual * precond),
                        jnp.sum(precond * precond_image),
                        jnp.sum(precond * image),
                        jnp.sum(direction * precond_image),
                    )
                )
            )
            gamma = sums[0]
            beta = gamma / gamma_prev
            curvature = sums[1] + beta * (sums[2] + sums[3]) + beta * beta * curvature_prev
            direction = precond + beta * direction
            image = precond_image + beta * image
        alpha = gamma / curvature
        solution = solution + alpha * direction
        residual = residual - alpha * image
        gamma_prev, curvature_prev = gamma, curvature
    return (solution, residual, direction)


def solution(mesh):
    in_specs = (P(None, "py", "px"), P(None, "py", "px"), P(None, "py", "px"), P(), P(), P(), P())
    out_specs = (P(None, "py", "px"), P(None, "py", "px"), P(None, "py", "px"))
    return jax.shard_map(shards, mesh=mesh, in_specs=in_specs, out_specs=out_specs, check_vma=False)
```

```python
import jax
import jax.numpy as jnp
from jax import lax
from jax.sharding import PartitionSpec as P

ITERS = 2


def padded_2(array, sides, width, interior=None, edge_map=None):
    result = array if interior is None else interior
    for axis, dim in sides:
        size, length = (lax.axis_size(axis), array.shape[dim])
        up = [(i, (i + 1) % size) for i in range(size - 1)]
        down = [(j, i) for i, j in up]
        last = lax.slice_in_dim(array, length - width, length, axis=dim)
        initial = lax.slice_in_dim(array, 0, width, axis=dim)
        before = lax.ppermute(last, axis, up)
        after = lax.ppermute(initial, axis, down)
        array = jnp.concatenate([before, array, after], axis=dim)
        if edge_map is None:
            result = array
        else:
            result = jnp.concatenate([edge_map(before), result, edge_map(after)], axis=dim)
    return result


def lookup(labels, table):
    values = jnp.zeros(labels.shape, table.dtype)
    for label in range(table.shape[0]):
        values = jnp.where(labels == label, table[label], values)
    return values


def for_sending(array):

    def short(part):
        return part.astype(jnp.bfloat16) if part.dtype == jnp.float32 else part

    return jax.tree.map(short, array)


def all_sum(values):
    axes = ("px", "py")
    count = lax.axis_size(axes)
    spread = jnp.broadcast_to(values[None], (count,) + values.shape)
    return jnp.sum(lax.all_to_all(spread, axes, 0, 0, tiled=True), 0)


def face_sum(padded, coeff_pad):
    values = padded[:, 1:-1, 1:-1]
    coeff = coeff_pad[:, 1:-1, 1:-1]
    height = values.shape[1]
    width = values.shape[2]
    result = jnp.zeros_like(values)
    for shift_y, shift_x in ((0, 1), (2, 1), (1, 0), (1, 2)):
        neighbour = padded[:, shift_y : shift_y + height, shift_x : shift_x + width]
        other = coeff_pad[:, shift_y : shift_y + height, shift_x : shift_x + width]
        result = result + 0.5 * (coeff + other) * (values - neighbour)
    vertical = 0.5 * (coeff[:-1] + coeff[1:]) * (values[:-1] - values[1:])
    zero_layer = jnp.zeros_like(values[:1])
    result = (
        result
        + jnp.concatenate((vertical, zero_layer), 0)
        - jnp.concatenate((zero_layer, vertical), 0)
    )
    return result


def exchange(block, axis, split_axis, concat_axis):
    size = lax.axis_size(axis)
    me = lax.axis_index(axis)
    piece = block.shape[split_axis] // size
    width = block.shape[concat_axis]
    shape = list(block.shape)
    shape[split_axis] = piece
    shape[concat_axis] = width * size
    result = jnp.zeros(shape, block.dtype)
    for shift in range(size):
        part = lax.dynamic_slice_in_dim(block, ((me + shift) % size) * piece, piece, split_axis)
        if shift:
            part = lax.ppermute(part, axis, [(i, (i + shift) % size) for i in range(size)])
        result = lax.dynamic_update_slice_in_dim(
            result, part, ((me - shift) % size) * width, concat_axis
        )
    return result


def precondition_lines(lines, first_level, eigenvectors, eigenvalues, level_shift):
    across = lax.axis_size("py")
    levels_here, rows, width = lines.shape
    cols = width // across
    first = jnp.dot(
        lines.reshape(levels_here * rows, width), eigenvectors, preferred_element_type=jnp.float32
    ).astype(jnp.bfloat16)
    outgoing = first.reshape(levels_here * rows, across, cols).transpose(1, 0, 2)
    incoming = lax.all_to_all(outgoing, "py", 0, 0, tiled=True)
    spectral = incoming.reshape(across, levels_here, rows, cols).transpose(1, 0, 2, 3)
    spectral = spectral.reshape(levels_here, across * rows, cols)
    second = jnp.einsum("jy,kyi->kji", eigenvectors, spectral, preferred_element_type=jnp.float32)
    eigen_cols = lax.dynamic_slice_in_dim(eigenvalues, lax.axis_index("py") * cols, cols, 0)
    shift_here = lax.dynamic_slice_in_dim(
        level_shift, first_level + lax.axis_index("px") * levels_here, levels_here, 0
    )
    denom = eigenvalues[None, :, None] + eigen_cols[None, None, :] + shift_here[:, None, None]
    scaled = (second / denom).astype(jnp.bfloat16)
    fourth = jnp.einsum(
        "yj,kji->kyi", eigenvectors, scaled, preferred_element_type=jnp.float32
    ).astype(jnp.bfloat16)
    outgoing = fourth.reshape(levels_here, across, rows, cols).transpose(1, 0, 2, 3)
    returned = lax.all_to_all(outgoing, "py", 0, 0, tiled=True)
    pencil = jnp.einsum(
        "qkyi,qix->kyx",
        returned,
        eigenvectors.reshape(across, cols, width),
        preferred_element_type=jnp.float32,
    )
    return exchange(pencil.astype(jnp.bfloat16), "px", 2, 0).astype(jnp.float32)


def precondition(residual, eigenvectors, eigenvalues, level_shift):
    levels = residual.shape[0]
    chunk = lax.axis_size("px")
    if levels % chunk or levels == chunk:
        chunk = levels
    parts = []
    waiting = residual
    for start in range(0, levels, chunk):
        lines = exchange(waiting[start : start + chunk].astype(jnp.bfloat16), "px", 0, 2)
        lines, waiting = lax.optimization_barrier((lines, waiting))
        parts.append(precondition_lines(lines, start, eigenvectors, eigenvalues, level_shift))
    return jnp.concatenate(parts, 0)


def operator(field, coeff_pad):
    padded = padded_2(for_sending(field), (("px", 2), ("py", 1)), 1).astype(field.dtype)
    return face_sum(padded, coeff_pad)


def shards(right_side, solution_in, classes, coeff_table, eigenvectors, eigenvalues, level_shift):
    table = coeff_table.astype(jnp.bfloat16)
    rounded = solution_in.astype(jnp.bfloat16)
    labels = classes.astype(jnp.bfloat16)
    stacked = padded_2(
        jnp.stack((rounded, labels)),
        (("px", 3), ("py", 2)),
        1,
        interior=jnp.stack((rounded, lookup(labels, table))),
        edge_map=lambda slab: jnp.stack((slab[0], lookup(slab[1], table))),
    ).astype(jnp.float32)
    coeff_pad = stacked[1]
    solution = solution_in
    residual = right_side - face_sum(stacked[0], coeff_pad)
    direction = image = None
    gamma_prev = curvature_prev = None
    for iteration in range(ITERS):
        precond = precondition(residual, eigenvectors, eigenvalues, level_shift)
        precond_image = operator(precond, coeff_pad)
        if iteration == 0:
            sums = all_sum(jnp.stack((jnp.sum(residual * precond), jnp.sum(precond * precond_image))))
            gamma, curvature = sums[0], sums[1]
            direction, image = precond, precond_image
        else:
            sums = all_sum(
                jnp.stack(
                    (
                        jnp.sum(residual * precond),
                        jnp.sum(precond * precond_image),
                        jnp.sum(precond * image),
                        jnp.sum(direction * precond_image),
                    )
                )
            )
            gamma = sums[0]
            beta = gamma / gamma_prev
            curvature = sums[1] + beta * (sums[2] + sums[3]) + beta * beta * curvature_prev
            direction = precond + beta * direction
            image = precond_image + beta * image
        alpha = gamma / curvature
        solution = solution + alpha * direction
        residual = residual - alpha * image
        gamma_prev, curvature_prev = gamma, curvature
    return (solution, residual, direction)


def solution(mesh):
    in_specs = (P(None, "py", "px"), P(None, "py", "px"), P(None, "py", "px"), P(), P(), P(), P())
    out_specs = (P(None, "py", "px"), P(None, "py", "px"), P(None, "py", "px"))
    return jax.shard_map(shards, mesh=mesh, in_specs=in_specs, out_specs=out_specs, check_vma=False)
```

```python
import jax
import jax.numpy as jnp
from jax import lax
from jax.sharding import PartitionSpec as P

ITERS = 2


def padded_2(array, sides, width):
    slabs = {}
    for axis, dim in sides:
        size, length = (lax.axis_size(axis), array.shape[dim])
        up = [(i, (i + 1) % size) for i in range(size - 1)]
        down = [(j, i) for i, j in up]
        last = lax.slice_in_dim(array, length - width, length, axis=dim)
        initial = lax.slice_in_dim(array, 0, width, axis=dim)
        slabs[dim] = (lax.ppermute(last, axis, up), lax.ppermute(initial, axis, down))
    for position, (axis, dim) in enumerate(sides):
        before, after = slabs[dim]
        for _, other in sides[:position]:
            pad = [(0, 0)] * array.ndim
            pad[other] = (width, width)
            before = jnp.pad(before, pad)
            after = jnp.pad(after, pad)
        array = jnp.concatenate([before, array, after], axis=dim)
    return array


def for_sending(array):

    def short(part):
        return part.astype(jnp.bfloat16) if part.dtype == jnp.float32 else part

    return jax.tree.map(short, array)


def all_sum(values):
    axes = ("px", "py")
    count = lax.axis_size(axes)
    spread = jnp.broadcast_to(values[None], (count,) + values.shape)
    return jnp.sum(lax.all_to_all(spread, axes, 0, 0, tiled=True), 0)


def face_sum(padded, coeff_pad):
    values = padded[:, 1:-1, 1:-1]
    coeff = coeff_pad[:, 1:-1, 1:-1]
    height = values.shape[1]
    width = values.shape[2]
    result = jnp.zeros_like(values)
    for shift_y, shift_x in ((0, 1), (2, 1), (1, 0), (1, 2)):
        neighbour = padded[:, shift_y : shift_y + height, shift_x : shift_x + width]
        other = coeff_pad[:, shift_y : shift_y + height, shift_x : shift_x + width]
        result = result + 0.5 * (coeff + other) * (values - neighbour)
    vertical = 0.5 * (coeff[:-1] + coeff[1:]) * (values[:-1] - values[1:])
    zero_layer = jnp.zeros_like(values[:1])
    result = (
        result
        + jnp.concatenate((vertical, zero_layer), 0)
        - jnp.concatenate((zero_layer, vertical), 0)
    )
    return result


def exchange(block, axis, split_axis, concat_axis):
    size = lax.axis_size(axis)
    me = lax.axis_index(axis)
    piece = block.shape[split_axis] // size
    width = block.shape[concat_axis]
    shape = list(block.shape)
    shape[split_axis] = piece
    shape[concat_axis] = width * size
    result = jnp.zeros(shape, block.dtype)
    for shift in range(size):
        part = lax.dynamic_slice_in_dim(block, ((me + shift) % size) * piece, piece, split_axis)
        if shift:
            part = lax.ppermute(part, axis, [(i, (i + shift) % size) for i in range(size)])
        result = lax.dynamic_update_slice_in_dim(
            result, part, ((me - shift) % size) * width, concat_axis
        )
    return result


def precondition_lines(lines, first_level, eigenvectors, eigenvalues, level_shift):
    across = lax.axis_size("py")
    levels_here, rows, width = lines.shape
    cols = width // across
    first = jnp.dot(
        lines.reshape(levels_here * rows, width), eigenvectors, preferred_element_type=jnp.float32
    ).astype(jnp.bfloat16)
    outgoing = first.reshape(levels_here * rows, across, cols).transpose(1, 0, 2)
    incoming = lax.all_to_all(outgoing, "py", 0, 0, tiled=True)
    spectral = incoming.reshape(across, levels_here, rows, cols).transpose(1, 0, 2, 3)
    spectral = spectral.reshape(levels_here, across * rows, cols)
    second = jnp.einsum("jy,kyi->kji", eigenvectors, spectral, preferred_element_type=jnp.float32)
    eigen_cols = lax.dynamic_slice_in_dim(eigenvalues, lax.axis_index("py") * cols, cols, 0)
    shift_here = lax.dynamic_slice_in_dim(
        level_shift, first_level + lax.axis_index("px") * levels_here, levels_here, 0
    )
    denom = eigenvalues[None, :, None] + eigen_cols[None, None, :] + shift_here[:, None, None]
    scaled = (second / denom).astype(jnp.bfloat16)
    fourth = jnp.einsum(
        "yj,kji->kyi", eigenvectors, scaled, preferred_element_type=jnp.float32
    ).astype(jnp.bfloat16)
    outgoing = fourth.reshape(levels_here, across, rows, cols).transpose(1, 0, 2, 3)
    returned = lax.all_to_all(outgoing, "py", 0, 0, tiled=True)
    pencil = jnp.einsum(
        "qkyi,qix->kyx",
        returned,
        eigenvectors.reshape(across, cols, width),
        preferred_element_type=jnp.float32,
    )
    return exchange(pencil.astype(jnp.bfloat16), "px", 2, 0).astype(jnp.float32)


def precondition(residual, eigenvectors, eigenvalues, level_shift):
    levels = residual.shape[0]
    chunk = lax.axis_size("px")
    if levels % chunk or levels == chunk:
        chunk = levels
    parts = []
    waiting = residual
    for start in range(0, levels, chunk):
        lines = exchange(waiting[start : start + chunk].astype(jnp.bfloat16), "px", 0, 2)
        lines, waiting = lax.optimization_barrier((lines, waiting))
        parts.append(precondition_lines(lines, start, eigenvectors, eigenvalues, level_shift))
    return jnp.concatenate(parts, 0)


def operator(field, coeff_pad):
    padded = padded_2(for_sending(field), (("px", 2), ("py", 1)), 1).astype(field.dtype)
    return face_sum(padded, coeff_pad)


def shards(right_side, solution_in, classes, coeff_table, eigenvectors, eigenvalues, level_shift):
    coeff = jnp.zeros(classes.shape, jnp.float32)
    for label in range(coeff_table.shape[0]):
        coeff = jnp.where(classes == label, coeff_table[label], coeff)
    stacked = padded_2(
        jnp.stack((solution_in, coeff)).astype(jnp.bfloat16), (("px", 3), ("py", 2)), 1
    ).astype(jnp.float32)
    coeff_pad = stacked[1]
    solution = solution_in
    levels = right_side.shape[0]
    chunk = lax.axis_size("px")
    if levels % chunk or levels == chunk:
        chunk = levels
    pieces = []
    for start in range(0, levels, chunk):
        low, high = max(start - 1, 0), min(start + chunk + 1, levels)
        image = face_sum(stacked[0, low:high], coeff_pad[low:high])
        pieces.append(right_side[start : start + chunk] - image[start - low : start - low + chunk])
    residual = jnp.concatenate(pieces, 0)
    direction = image = None
    gamma_prev = curvature_prev = None
    for iteration in range(ITERS):
        precond = precondition(residual, eigenvectors, eigenvalues, level_shift)
        precond_image = operator(precond, coeff_pad)
        if iteration == 0:
            sums = all_sum(jnp.stack((jnp.sum(residual * precond), jnp.sum(precond * precond_image))))
            gamma, curvature = sums[0], sums[1]
            direction, image = precond, precond_image
        else:
            sums = all_sum(
                jnp.stack(
                    (
                        jnp.sum(residual * precond),
                        jnp.sum(precond * precond_image),
                        jnp.sum(precond * image),
                        jnp.sum(direction * precond_image),
                    )
                )
            )
            gamma = sums[0]
            beta = gamma / gamma_prev
            curvature = sums[1] + beta * (sums[2] + sums[3]) + beta * beta * curvature_prev
            direction = precond + beta * direction
            image = precond_image + beta * image
        alpha = gamma / curvature
        solution = solution + alpha * direction
        residual = residual - alpha * image
        gamma_prev, curvature_prev = gamma, curvature
    return (solution, residual, direction)


def solution(mesh):
    in_specs = (P(None, "py", "px"), P(None, "py", "px"), P(None, "py", "px"), P(), P(), P(), P())
    out_specs = (P(None, "py", "px"), P(None, "py", "px"), P(None, "py", "px"))
    return jax.shard_map(shards, mesh=mesh, in_specs=in_specs, out_specs=out_specs, check_vma=False)
```

```python
import jax
import jax.numpy as jnp
from jax import lax
from jax.sharding import PartitionSpec as P

ITERS = 2


def padded_2(array, sides, width):
    slabs = {}
    for axis, dim in sides:
        size, length = (lax.axis_size(axis), array.shape[dim])
        up = [(i, (i + 1) % size) for i in range(size - 1)]
        down = [(j, i) for i, j in up]
        last = lax.slice_in_dim(array, length - width, length, axis=dim)
        initial = lax.slice_in_dim(array, 0, width, axis=dim)
        slabs[dim] = (lax.ppermute(last, axis, up), lax.ppermute(initial, axis, down))
    for position, (axis, dim) in enumerate(sides):
        before, after = slabs[dim]
        for _, other in sides[:position]:
            pad = [(0, 0)] * array.ndim
            pad[other] = (width, width)
            before = jnp.pad(before, pad)
            after = jnp.pad(after, pad)
        array = jnp.concatenate([before, array, after], axis=dim)
    return array


def for_sending(array):

    def short(part):
        return part.astype(jnp.bfloat16) if part.dtype == jnp.float32 else part

    return jax.tree.map(short, array)


def all_sum(values):
    axes = ("px", "py")
    count = lax.axis_size(axes)
    spread = jnp.broadcast_to(values[None], (count,) + values.shape)
    return jnp.sum(lax.all_to_all(spread, axes, 0, 0, tiled=True), 0)


def face_sum(padded, coeff_pad):
    values = padded[:, 1:-1, 1:-1]
    coeff = coeff_pad[:, 1:-1, 1:-1]
    height = values.shape[1]
    width = values.shape[2]
    result = jnp.zeros_like(values)
    for shift_y, shift_x in ((0, 1), (2, 1), (1, 0), (1, 2)):
        neighbour = padded[:, shift_y : shift_y + height, shift_x : shift_x + width]
        other = coeff_pad[:, shift_y : shift_y + height, shift_x : shift_x + width]
        result = result + 0.5 * (coeff + other) * (values - neighbour)
    vertical = 0.5 * (coeff[:-1] + coeff[1:]) * (values[:-1] - values[1:])
    zero_layer = jnp.zeros_like(values[:1])
    result = (
        result
        + jnp.concatenate((vertical, zero_layer), 0)
        - jnp.concatenate((zero_layer, vertical), 0)
    )
    return result


def exchange(block, axis, split_axis, concat_axis):
    size = lax.axis_size(axis)
    me = lax.axis_index(axis)
    piece = block.shape[split_axis] // size
    width = block.shape[concat_axis]
    shape = list(block.shape)
    shape[split_axis] = piece
    shape[concat_axis] = width * size
    result = jnp.zeros(shape, block.dtype)
    for shift in range(size):
        part = lax.dynamic_slice_in_dim(block, ((me + shift) % size) * piece, piece, split_axis)
        if shift:
            part = lax.ppermute(part, axis, [(i, (i + shift) % size) for i in range(size)])
        result = lax.dynamic_update_slice_in_dim(
            result, part, ((me - shift) % size) * width, concat_axis
        )
    return result


def precondition_lines(lines, first_level, eigenvectors, eigenvalues, level_shift):
    across = lax.axis_size("py")
    levels_here, rows, width = lines.shape
    cols = width // across
    first = jnp.dot(
        lines.reshape(levels_here * rows, width), eigenvectors, preferred_element_type=jnp.float32
    ).astype(jnp.bfloat16)
    outgoing = first.reshape(levels_here * rows, across, cols).transpose(1, 0, 2)
    incoming = lax.all_to_all(outgoing, "py", 0, 0, tiled=True)
    spectral = incoming.reshape(across, levels_here, rows, cols).transpose(1, 0, 2, 3)
    spectral = spectral.reshape(levels_here, across * rows, cols)
    second = jnp.einsum("jy,kyi->kji", eigenvectors, spectral, preferred_element_type=jnp.float32)
    eigen_cols = lax.dynamic_slice_in_dim(eigenvalues, lax.axis_index("py") * cols, cols, 0)
    shift_here = lax.dynamic_slice_in_dim(
        level_shift, first_level + lax.axis_index("px") * levels_here, levels_here, 0
    )
    denom = eigenvalues[None, :, None] + eigen_cols[None, None, :] + shift_here[:, None, None]
    scaled = (second / denom).astype(jnp.bfloat16)
    fourth = jnp.einsum(
        "yj,kji->kyi", eigenvectors, scaled, preferred_element_type=jnp.float32
    ).astype(jnp.bfloat16)
    outgoing = fourth.reshape(levels_here, across, rows, cols).transpose(1, 0, 2, 3)
    returned = lax.all_to_all(outgoing, "py", 0, 0, tiled=True)
    pencil = jnp.einsum(
        "qkyi,qix->kyx",
        returned,
        eigenvectors.reshape(across, cols, width),
        preferred_element_type=jnp.float32,
    )
    return return_lines(pencil.astype(jnp.bfloat16))


def precondition(residual, eigenvectors, eigenvalues, level_shift):
    levels = residual.shape[0]
    chunk = lax.axis_size("px")
    if levels % chunk or levels == chunk:
        chunk = levels
    parts = []
    waiting = residual
    for start in range(0, levels, chunk):
        lines = exchange(waiting[start : start + chunk].astype(jnp.bfloat16), "px", 0, 2)
        lines, waiting = lax.optimization_barrier((lines, waiting))
        parts.append(precondition_lines(lines, start, eigenvectors, eigenvalues, level_shift))
    return jnp.concatenate(parts, 0)


def return_lines(pencil):
    size = lax.axis_size("px")
    me = lax.axis_index("px")
    levels_here, rows, width = pencil.shape
    piece = width // size
    padded = jnp.pad(pencil, ((0, 0), (0, 0), (1, 1)))
    result = jnp.zeros((levels_here * size, rows, piece + 2), pencil.dtype)
    for shift in range(size):
        part = lax.dynamic_slice_in_dim(padded, ((me + shift) % size) * piece, piece + 2, 2)
        if shift:
            part = lax.ppermute(part, "px", [(i, (i + shift) % size) for i in range(size)])
        result = lax.dynamic_update_slice_in_dim(
            result, part, ((me - shift) % size) * levels_here, 0
        )
    return result


def operator(wide, coeff_pad):
    padded = padded_2(wide, (("py", 1),), 1).astype(jnp.float32)
    return face_sum(padded, coeff_pad)


def shards(right_side, solution_in, classes, coeff_table, eigenvectors, eigenvalues, level_shift):
    coeff = jnp.zeros(classes.shape, jnp.float32)
    for label in range(coeff_table.shape[0]):
        coeff = jnp.where(classes == label, coeff_table[label], coeff)
    stacked = padded_2(
        jnp.stack((solution_in, coeff)).astype(jnp.bfloat16), (("px", 3), ("py", 2)), 1
    ).astype(jnp.float32)
    coeff_pad = stacked[1]
    solution = solution_in
    residual = right_side - face_sum(stacked[0], coeff_pad)
    direction = image = None
    gamma_prev = curvature_prev = None
    for iteration in range(ITERS):
        wide = precondition(residual, eigenvectors, eigenvalues, level_shift)
        precond = wide[:, :, 1:-1].astype(jnp.float32)
        precond_image = operator(wide, coeff_pad)
        if iteration == 0:
            sums = all_sum(jnp.stack((jnp.sum(residual * precond), jnp.sum(precond * precond_image))))
            gamma, curvature = sums[0], sums[1]
            direction, image = precond, precond_image
        else:
            sums = all_sum(
                jnp.stack(
                    (
                        jnp.sum(residual * precond),
                        jnp.sum(precond * precond_image),
                        jnp.sum(precond * image),
                        jnp.sum(direction * precond_image),
                    )
                )
            )
            gamma = sums[0]
            beta = gamma / gamma_prev
            curvature = sums[1] + beta * (sums[2] + sums[3]) + beta * beta * curvature_prev
            direction = precond + beta * direction
            image = precond_image + beta * image
        alpha = gamma / curvature
        solution = solution + alpha * direction
        residual = residual - alpha * image
        gamma_prev, curvature_prev = gamma, curvature
    return (solution, residual, direction)


def solution(mesh):
    in_specs = (P(None, "py", "px"), P(None, "py", "px"), P(None, "py", "px"), P(), P(), P(), P())
    out_specs = (P(None, "py", "px"), P(None, "py", "px"), P(None, "py", "px"))
    return jax.shard_map(shards, mesh=mesh, in_specs=in_specs, out_specs=out_specs, check_vma=False)
```

```python
import jax
import jax.numpy as jnp
from jax import lax
from jax.sharding import PartitionSpec as P

ITERS = 2


def padded_2(array, sides, width):
    slabs = {}
    for axis, dim in sides:
        size, length = (lax.axis_size(axis), array.shape[dim])
        up = [(i, (i + 1) % size) for i in range(size - 1)]
        down = [(j, i) for i, j in up]
        last = lax.slice_in_dim(array, length - width, length, axis=dim)
        initial = lax.slice_in_dim(array, 0, width, axis=dim)
        slabs[dim] = (lax.ppermute(last, axis, up), lax.ppermute(initial, axis, down))
    for position, (axis, dim) in enumerate(sides):
        before, after = slabs[dim]
        for _, other in sides[:position]:
            pad = [(0, 0)] * array.ndim
            pad[other] = (width, width)
            before = jnp.pad(before, pad)
            after = jnp.pad(after, pad)
        array = jnp.concatenate([before, array, after], axis=dim)
    return array


def for_sending(array):

    def short(part):
        return part.astype(jnp.bfloat16) if part.dtype == jnp.float32 else part

    return jax.tree.map(short, array)


def all_sum(values):
    axes = ("px", "py")
    count = lax.axis_size(axes)
    spread = jnp.broadcast_to(values[None], (count,) + values.shape)
    return jnp.sum(lax.all_to_all(spread, axes, 0, 0, tiled=True), 0)


def face_sum(padded, coeff_pad):
    values = padded[:, 1:-1, 1:-1]
    coeff = coeff_pad[:, 1:-1, 1:-1]
    height = values.shape[1]
    width = values.shape[2]
    result = jnp.zeros_like(values)
    for shift_y, shift_x in ((0, 1), (2, 1), (1, 0), (1, 2)):
        neighbour = padded[:, shift_y : shift_y + height, shift_x : shift_x + width]
        other = coeff_pad[:, shift_y : shift_y + height, shift_x : shift_x + width]
        result = result + 0.5 * (coeff + other) * (values - neighbour)
    vertical = 0.5 * (coeff[:-1] + coeff[1:]) * (values[:-1] - values[1:])
    zero_layer = jnp.zeros_like(values[:1])
    result = (
        result
        + jnp.concatenate((vertical, zero_layer), 0)
        - jnp.concatenate((zero_layer, vertical), 0)
    )
    return result


def exchange(block, axis, split_axis, concat_axis):
    size = lax.axis_size(axis)
    me = lax.axis_index(axis)
    piece = block.shape[split_axis] // size
    width = block.shape[concat_axis]
    shape = list(block.shape)
    shape[split_axis] = piece
    shape[concat_axis] = width * size
    result = jnp.zeros(shape, block.dtype)
    for shift in range(size):
        part = lax.dynamic_slice_in_dim(block, ((me + shift) % size) * piece, piece, split_axis)
        if shift:
            part = lax.ppermute(part, axis, [(i, (i + shift) % size) for i in range(size)])
        result = lax.dynamic_update_slice_in_dim(
            result, part, ((me - shift) % size) * width, concat_axis
        )
    return result


def precondition_lines(lines, first_level, eigenvectors, eigenvalues, level_shift):
    across = lax.axis_size("py")
    levels_here, rows, width = lines.shape
    cols = width // across
    first = jnp.dot(
        lines.reshape(levels_here * rows, width), eigenvectors, preferred_element_type=jnp.float32
    ).astype(jnp.bfloat16)
    outgoing = first.reshape(levels_here * rows, across, cols).transpose(1, 0, 2)
    incoming = lax.all_to_all(outgoing, "py", 0, 0, tiled=True)
    spectral = incoming.reshape(across, levels_here, rows, cols).transpose(1, 0, 2, 3)
    spectral = spectral.reshape(levels_here, across * rows, cols)
    second = jnp.einsum("jy,kyi->kji", eigenvectors, spectral, preferred_element_type=jnp.float32)
    eigen_cols = lax.dynamic_slice_in_dim(eigenvalues, lax.axis_index("py") * cols, cols, 0)
    shift_here = lax.dynamic_slice_in_dim(
        level_shift, first_level + lax.axis_index("px") * levels_here, levels_here, 0
    )
    denom = eigenvalues[None, :, None] + eigen_cols[None, None, :] + shift_here[:, None, None]
    scaled = (second / denom).astype(jnp.bfloat16)
    fourth = jnp.einsum(
        "yj,kji->kyi", eigenvectors, scaled, preferred_element_type=jnp.float32
    ).astype(jnp.bfloat16)
    edged = jnp.pad(fourth, ((0, 0), (1, 1), (0, 0)))
    outgoing = jnp.stack(
        [edged[:, target * rows : target * rows + rows + 2] for target in range(across)], 0
    )
    returned = lax.all_to_all(outgoing, "py", 0, 0, tiled=True)
    pencil = jnp.einsum(
        "qkyi,qix->kyx",
        returned,
        eigenvectors.reshape(across, cols, width),
        preferred_element_type=jnp.float32,
    )
    return return_lines(pencil.astype(jnp.bfloat16))


def precondition(residual, eigenvectors, eigenvalues, level_shift):
    levels = residual.shape[0]
    chunk = lax.axis_size("px")
    if levels % chunk or levels == chunk:
        chunk = levels
    parts = []
    waiting = residual
    for start in range(0, levels, chunk):
        lines = exchange(waiting[start : start + chunk].astype(jnp.bfloat16), "px", 0, 2)
        lines, waiting = lax.optimization_barrier((lines, waiting))
        parts.append(precondition_lines(lines, start, eigenvectors, eigenvalues, level_shift))
    return jnp.concatenate(parts, 0)


def return_lines(pencil):
    size = lax.axis_size("px")
    me = lax.axis_index("px")
    levels_here, rows, width = pencil.shape
    piece = width // size
    padded = jnp.pad(pencil, ((0, 0), (0, 0), (1, 1)))
    result = jnp.zeros((levels_here * size, rows, piece + 2), pencil.dtype)
    for shift in range(size):
        part = lax.dynamic_slice_in_dim(padded, ((me + shift) % size) * piece, piece + 2, 2)
        if shift:
            part = lax.ppermute(part, "px", [(i, (i + shift) % size) for i in range(size)])
        result = lax.dynamic_update_slice_in_dim(
            result, part, ((me - shift) % size) * levels_here, 0
        )
    return result


def operator(wide, coeff_pad):
    return face_sum(wide.astype(jnp.float32), coeff_pad)


def shards(right_side, solution_in, classes, coeff_table, eigenvectors, eigenvalues, level_shift):
    coeff = jnp.zeros(classes.shape, jnp.float32)
    for label in range(coeff_table.shape[0]):
        coeff = jnp.where(classes == label, coeff_table[label], coeff)
    stacked = padded_2(
        jnp.stack((solution_in, coeff)).astype(jnp.bfloat16), (("px", 3), ("py", 2)), 1
    ).astype(jnp.float32)
    coeff_pad = stacked[1]
    solution = solution_in
    residual = right_side - face_sum(stacked[0], coeff_pad)
    direction = image = None
    gamma_prev = curvature_prev = None
    for iteration in range(ITERS):
        wide = precondition(residual, eigenvectors, eigenvalues, level_shift)
        precond = wide[:, 1:-1, 1:-1].astype(jnp.float32)
        precond_image = operator(wide, coeff_pad)
        if iteration == 0:
            sums = all_sum(jnp.stack((jnp.sum(residual * precond), jnp.sum(precond * precond_image))))
            gamma, curvature = sums[0], sums[1]
            direction, image = precond, precond_image
        else:
            sums = all_sum(
                jnp.stack(
                    (
                        jnp.sum(residual * precond),
                        jnp.sum(precond * precond_image),
                        jnp.sum(precond * image),
                        jnp.sum(direction * precond_image),
                    )
                )
            )
            gamma = sums[0]
            beta = gamma / gamma_prev
            curvature = sums[1] + beta * (sums[2] + sums[3]) + beta * beta * curvature_prev
            direction = precond + beta * direction
            image = precond_image + beta * image
        alpha = gamma / curvature
        solution = solution + alpha * direction
        residual = residual - alpha * image
        gamma_prev, curvature_prev = gamma, curvature
    return (solution, residual, direction)


def solution(mesh):
    in_specs = (P(None, "py", "px"), P(None, "py", "px"), P(None, "py", "px"), P(), P(), P(), P())
    out_specs = (P(None, "py", "px"), P(None, "py", "px"), P(None, "py", "px"))
    return jax.shard_map(shards, mesh=mesh, in_specs=in_specs, out_specs=out_specs, check_vma=False)
```

```python
import jax
import jax.numpy as jnp
from jax import lax
from jax.sharding import PartitionSpec as P

ITERS = 2


def padded_2(array, sides, width):
    slabs = {}
    for axis, dim in sides:
        size, length = (lax.axis_size(axis), array.shape[dim])
        up = [(i, (i + 1) % size) for i in range(size - 1)]
        down = [(j, i) for i, j in up]
        last = lax.slice_in_dim(array, length - width, length, axis=dim)
        initial = lax.slice_in_dim(array, 0, width, axis=dim)
        slabs[dim] = (lax.ppermute(last, axis, up), lax.ppermute(initial, axis, down))
    for position, (axis, dim) in enumerate(sides):
        before, after = slabs[dim]
        for _, other in sides[:position]:
            pad = [(0, 0)] * array.ndim
            pad[other] = (width, width)
            before = jnp.pad(before, pad)
            after = jnp.pad(after, pad)
        array = jnp.concatenate([before, array, after], axis=dim)
    return array


def for_sending(array):

    def short(part):
        return part.astype(jnp.bfloat16) if part.dtype == jnp.float32 else part

    return jax.tree.map(short, array)


def all_sum(values):
    axes = ("px", "py")
    count = lax.axis_size(axes)
    spread = jnp.broadcast_to(values[None], (count,) + values.shape)
    return jnp.sum(lax.all_to_all(spread, axes, 0, 0, tiled=True), 0)


def face_sum(padded, coeff_pad):
    values = padded[:, 1:-1, 1:-1]
    coeff = coeff_pad[:, 1:-1, 1:-1]
    height = values.shape[1]
    width = values.shape[2]
    result = jnp.zeros_like(values)
    for shift_y, shift_x in ((0, 1), (2, 1), (1, 0), (1, 2)):
        neighbour = padded[:, shift_y : shift_y + height, shift_x : shift_x + width]
        other = coeff_pad[:, shift_y : shift_y + height, shift_x : shift_x + width]
        result = result + 0.5 * (coeff + other) * (values - neighbour)
    vertical = 0.5 * (coeff[:-1] + coeff[1:]) * (values[:-1] - values[1:])
    zero_layer = jnp.zeros_like(values[:1])
    result = (
        result
        + jnp.concatenate((vertical, zero_layer), 0)
        - jnp.concatenate((zero_layer, vertical), 0)
    )
    return result


def exchange(block, axis, split_axis, concat_axis):
    size = lax.axis_size(axis)
    me = lax.axis_index(axis)
    piece = block.shape[split_axis] // size
    width = block.shape[concat_axis]
    shape = list(block.shape)
    shape[split_axis] = piece
    shape[concat_axis] = width * size
    result = jnp.zeros(shape, block.dtype)
    for shift in range(size):
        part = lax.dynamic_slice_in_dim(block, ((me + shift) % size) * piece, piece, split_axis)
        if shift:
            part = lax.ppermute(part, axis, [(i, (i + shift) % size) for i in range(size)])
        result = lax.dynamic_update_slice_in_dim(
            result, part, ((me - shift) % size) * width, concat_axis
        )
    return result


def precondition_lines(lines, first_level, eigenvectors, eigenvalues, level_shift):
    across = lax.axis_size("py")
    levels_here, rows, width = lines.shape
    cols = width // across
    first = jnp.dot(
        lines.reshape(levels_here * rows, width), eigenvectors, preferred_element_type=jnp.float32
    ).astype(jnp.bfloat16)
    outgoing = first.reshape(levels_here * rows, across, cols).transpose(1, 0, 2)
    incoming = lax.all_to_all(outgoing, "py", 0, 0, tiled=True)
    spectral = incoming.reshape(across, levels_here, rows, cols).transpose(1, 0, 2, 3)
    spectral = spectral.reshape(levels_here, across * rows, cols)
    second = jnp.einsum("jy,kyi->kji", eigenvectors, spectral, preferred_element_type=jnp.float32)
    eigen_cols = lax.dynamic_slice_in_dim(eigenvalues, lax.axis_index("py") * cols, cols, 0)
    shift_here = lax.dynamic_slice_in_dim(
        level_shift, first_level + lax.axis_index("px") * levels_here, levels_here, 0
    )
    denom = eigenvalues[None, :, None] + eigen_cols[None, None, :] + shift_here[:, None, None]
    scaled = (second / denom).astype(jnp.bfloat16)
    fourth = jnp.einsum(
        "yj,kji->kyi", eigenvectors, scaled, preferred_element_type=jnp.float32
    ).astype(jnp.bfloat16)
    edged = jnp.pad(fourth, ((0, 0), (1, 1), (0, 0)))
    outgoing = jnp.stack(
        [edged[:, target * rows : target * rows + rows + 2] for target in range(across)], 0
    )
    returned = lax.all_to_all(outgoing, "py", 0, 0, tiled=True)
    pencil = jnp.einsum(
        "qkyi,qix->kyx",
        returned,
        eigenvectors.reshape(across, cols, width),
        preferred_element_type=jnp.float32,
    )
    return return_lines(pencil.astype(jnp.bfloat16))


def precondition(residual, eigenvectors, eigenvalues, level_shift):
    levels = residual.shape[0]
    chunk = lax.axis_size("px")
    if levels % chunk or levels == chunk:
        chunk = levels
    parts = []
    waiting = residual
    for start in range(0, levels, chunk):
        lines = exchange(waiting[start : start + chunk].astype(jnp.bfloat16), "px", 0, 2)
        lines, waiting = lax.optimization_barrier((lines, waiting))
        parts.append(precondition_lines(lines, start, eigenvectors, eigenvalues, level_shift))
    return jnp.concatenate(parts, 0)


def return_lines(pencil):
    size = lax.axis_size("px")
    me = lax.axis_index("px")
    levels_here, rows, width = pencil.shape
    piece = width // size
    padded = jnp.pad(pencil, ((0, 0), (0, 0), (1, 1)))
    result = jnp.zeros((levels_here * size, rows, piece + 2), pencil.dtype)
    for shift in range(size):
        part = lax.dynamic_slice_in_dim(padded, ((me + shift) % size) * piece, piece + 2, 2)
        if shift:
            part = lax.ppermute(part, "px", [(i, (i + shift) % size) for i in range(size)])
        result = lax.dynamic_update_slice_in_dim(
            result, part, ((me - shift) % size) * levels_here, 0
        )
    return result


def operator(wide, coeff_pad):
    return face_sum(wide.astype(jnp.float32), coeff_pad)


def shards(right_side, solution_in, classes, coeff_table, eigenvectors, eigenvalues, level_shift):
    labels = classes.astype(jnp.bfloat16)
    table = coeff_table.astype(jnp.bfloat16)
    coeff = jnp.zeros(classes.shape, jnp.bfloat16)
    for label in range(coeff_table.shape[0]):
        coeff = jnp.where(labels == label, table[label], coeff)
    stacked = padded_2(
        jnp.stack((solution_in, coeff)).astype(jnp.bfloat16), (("px", 3), ("py", 2)), 1
    ).astype(jnp.float32)
    coeff_pad = stacked[1]
    solution = solution_in
    residual = right_side - face_sum(stacked[0], coeff_pad)
    direction = image = None
    gamma_prev = curvature_prev = None
    for iteration in range(ITERS):
        wide = precondition(residual, eigenvectors, eigenvalues, level_shift)
        precond = wide[:, 1:-1, 1:-1].astype(jnp.float32)
        precond_image = operator(wide, coeff_pad)
        if iteration == 0:
            sums = all_sum(jnp.stack((jnp.sum(residual * precond), jnp.sum(precond * precond_image))))
            gamma, curvature = sums[0], sums[1]
            direction, image = precond, precond_image
        else:
            sums = all_sum(
                jnp.stack(
                    (
                        jnp.sum(residual * precond),
                        jnp.sum(precond * precond_image),
                        jnp.sum(precond * image),
                        jnp.sum(direction * precond_image),
                    )
                )
            )
            gamma = sums[0]
            beta = gamma / gamma_prev
            curvature = sums[1] + beta * (sums[2] + sums[3]) + beta * beta * curvature_prev
            direction = precond + beta * direction
            image = precond_image + beta * image
        alpha = gamma / curvature
        solution = solution + alpha * direction
        residual = residual - alpha * image
        gamma_prev, curvature_prev = gamma, curvature
    return (solution, residual, direction)


def solution(mesh):
    in_specs = (P(None, "py", "px"), P(None, "py", "px"), P(None, "py", "px"), P(), P(), P(), P())
    out_specs = (P(None, "py", "px"), P(None, "py", "px"), P(None, "py", "px"))
    return jax.shard_map(shards, mesh=mesh, in_specs=in_specs, out_specs=out_specs, check_vma=False)
```

```python
import jax
import jax.numpy as jnp
from jax import lax
from jax.sharding import PartitionSpec as P

ITERS = 2


def padded_2(array, sides, width):
    slabs = {}
    for axis, dim in sides:
        size, length = (lax.axis_size(axis), array.shape[dim])
        up = [(i, (i + 1) % size) for i in range(size - 1)]
        down = [(j, i) for i, j in up]
        last = lax.slice_in_dim(array, length - width, length, axis=dim)
        initial = lax.slice_in_dim(array, 0, width, axis=dim)
        slabs[dim] = (lax.ppermute(last, axis, up), lax.ppermute(initial, axis, down))
    for position, (axis, dim) in enumerate(sides):
        before, after = slabs[dim]
        for _, other in sides[:position]:
            pad = [(0, 0)] * array.ndim
            pad[other] = (width, width)
            before = jnp.pad(before, pad)
            after = jnp.pad(after, pad)
        array = jnp.concatenate([before, array, after], axis=dim)
    return array


def for_sending(array):

    def short(part):
        return part.astype(jnp.bfloat16) if part.dtype == jnp.float32 else part

    return jax.tree.map(short, array)


def all_sum(values):
    axes = ("px", "py")
    count = lax.axis_size(axes)
    spread = jnp.broadcast_to(values[None], (count,) + values.shape)
    return jnp.sum(lax.all_to_all(spread, axes, 0, 0, tiled=True), 0)


def face_sum(padded, coeff_pad):
    values = padded[:, 1:-1, 1:-1]
    coeff = coeff_pad[:, 1:-1, 1:-1]
    height = values.shape[1]
    width = values.shape[2]
    result = jnp.zeros_like(values)
    for shift_y, shift_x in ((0, 1), (2, 1), (1, 0), (1, 2)):
        neighbour = padded[:, shift_y : shift_y + height, shift_x : shift_x + width]
        other = coeff_pad[:, shift_y : shift_y + height, shift_x : shift_x + width]
        result = result + 0.5 * (coeff + other) * (values - neighbour)
    vertical = 0.5 * (coeff[:-1] + coeff[1:]) * (values[:-1] - values[1:])
    zero_layer = jnp.zeros_like(values[:1])
    result = (
        result
        + jnp.concatenate((vertical, zero_layer), 0)
        - jnp.concatenate((zero_layer, vertical), 0)
    )
    return result


def exchange(block, axis, split_axis, concat_axis):
    size = lax.axis_size(axis)
    me = lax.axis_index(axis)
    piece = block.shape[split_axis] // size
    width = block.shape[concat_axis]
    shape = list(block.shape)
    shape[split_axis] = piece
    shape[concat_axis] = width * size
    result = jnp.zeros(shape, block.dtype)
    for shift in range(size):
        part = lax.dynamic_slice_in_dim(block, ((me + shift) % size) * piece, piece, split_axis)
        if shift:
            part = lax.ppermute(part, axis, [(i, (i + shift) % size) for i in range(size)])
        result = lax.dynamic_update_slice_in_dim(
            result, part, ((me - shift) % size) * width, concat_axis
        )
    return result


def precondition_lines(lines, first_level, eigenvectors, eigenvalues, level_shift):
    across = lax.axis_size("py")
    levels_here, rows, width = lines.shape
    cols = width // across
    first = jnp.dot(
        lines.reshape(levels_here * rows, width), eigenvectors, preferred_element_type=jnp.float32
    ).astype(jnp.bfloat16)
    outgoing = first.reshape(levels_here * rows, across, cols).transpose(1, 0, 2)
    incoming = lax.all_to_all(outgoing, "py", 0, 0, tiled=True)
    spectral = incoming.reshape(across, levels_here, rows, cols).transpose(1, 0, 2, 3)
    spectral = spectral.reshape(levels_here, across * rows, cols)
    second = jnp.einsum("jy,kyi->kji", eigenvectors, spectral, preferred_element_type=jnp.float32)
    eigen_cols = lax.dynamic_slice_in_dim(eigenvalues, lax.axis_index("py") * cols, cols, 0)
    shift_here = lax.dynamic_slice_in_dim(
        level_shift, first_level + lax.axis_index("px") * levels_here, levels_here, 0
    )
    denom = eigenvalues[None, :, None] + eigen_cols[None, None, :] + shift_here[:, None, None]
    scaled = (second / denom).astype(jnp.bfloat16)
    fourth = jnp.einsum(
        "yj,kji->kyi", eigenvectors, scaled, preferred_element_type=jnp.float32
    ).astype(jnp.bfloat16)
    edged = jnp.pad(fourth, ((0, 0), (1, 1), (0, 0)))
    outgoing = jnp.stack(
        [edged[:, target * rows : target * rows + rows + 2] for target in range(across)], 0
    )
    returned = lax.all_to_all(outgoing, "py", 0, 0, tiled=True)
    pencil = jnp.einsum(
        "qkyi,qix->kyx",
        returned,
        eigenvectors.reshape(across, cols, width),
        preferred_element_type=jnp.float32,
    )
    return return_lines(pencil.astype(jnp.bfloat16))


def precondition(residual, eigenvectors, eigenvalues, level_shift):
    levels = residual.shape[0]
    chunk = lax.axis_size("px")
    if levels % chunk or levels == chunk:
        chunk = levels
    parts = []
    waiting = residual
    for start in range(0, levels, chunk):
        lines = exchange(waiting[start : start + chunk].astype(jnp.bfloat16), "px", 0, 2)
        lines, waiting = lax.optimization_barrier((lines, waiting))
        parts.append(precondition_lines(lines, start, eigenvectors, eigenvalues, level_shift))
    return jnp.concatenate(parts, 0)


def return_lines(pencil):
    size = lax.axis_size("px")
    me = lax.axis_index("px")
    levels_here, rows, width = pencil.shape
    piece = width // size
    padded = jnp.pad(pencil, ((0, 0), (0, 0), (1, 1)))
    result = jnp.zeros((levels_here * size, rows, piece + 2), pencil.dtype)
    for shift in range(size):
        part = lax.dynamic_slice_in_dim(padded, ((me + shift) % size) * piece, piece + 2, 2)
        if shift:
            part = lax.ppermute(part, "px", [(i, (i + shift) % size) for i in range(size)])
        result = lax.dynamic_update_slice_in_dim(
            result, part, ((me - shift) % size) * levels_here, 0
        )
    return result


def operator(wide, coeff_pad):
    return face_sum(wide.astype(jnp.float32), coeff_pad)


def shards(right_side, solution_in, classes, coeff_table, eigenvectors, eigenvalues, level_shift):
    labels = classes.astype(jnp.bfloat16)
    table = coeff_table.astype(jnp.bfloat16)
    coeff = jnp.zeros(classes.shape, jnp.bfloat16)
    for label in range(coeff_table.shape[0]):
        coeff = jnp.where(labels == label, table[label], coeff)
    stacked = padded_2(
        jnp.stack((solution_in, coeff)).astype(jnp.bfloat16), (("px", 3), ("py", 2)), 1
    )
    coeff_pad = stacked[1].astype(jnp.float32)
    solution = solution_in
    residual = right_side - face_sum(stacked[0].astype(jnp.float32), coeff_pad)
    direction = image = None
    gamma_prev = curvature_prev = None
    for iteration in range(ITERS):
        wide = precondition(residual, eigenvectors, eigenvalues, level_shift)
        precond = wide[:, 1:-1, 1:-1].astype(jnp.float32)
        precond_image = operator(wide, coeff_pad)
        if iteration == 0:
            sums = all_sum(jnp.stack((jnp.sum(residual * precond), jnp.sum(precond * precond_image))))
            gamma, curvature = sums[0], sums[1]
            direction, image = precond, precond_image
        else:
            sums = all_sum(
                jnp.stack(
                    (
                        jnp.sum(residual * precond),
                        jnp.sum(precond * precond_image),
                        jnp.sum(precond * image),
                        jnp.sum(direction * precond_image),
                    )
                )
            )
            gamma = sums[0]
            beta = gamma / gamma_prev
            curvature = sums[1] + beta * (sums[2] + sums[3]) + beta * beta * curvature_prev
            direction = precond + beta * direction
            image = precond_image + beta * image
        alpha = gamma / curvature
        solution = solution + alpha * direction
        residual = residual - alpha * image
        gamma_prev, curvature_prev = gamma, curvature
    return (solution, residual, direction)


def solution(mesh):
    in_specs = (P(None, "py", "px"), P(None, "py", "px"), P(None, "py", "px"), P(), P(), P(), P())
    out_specs = (P(None, "py", "px"), P(None, "py", "px"), P(None, "py", "px"))
    return jax.shard_map(shards, mesh=mesh, in_specs=in_specs, out_specs=out_specs, check_vma=False)
```

```python
import jax
import jax.numpy as jnp
from jax import lax
from jax.sharding import PartitionSpec as P

ITERS = 2


def padded_2(array, sides, width):
    slabs = {}
    for axis, dim in sides:
        size, length = (lax.axis_size(axis), array.shape[dim])
        up = [(i, (i + 1) % size) for i in range(size - 1)]
        down = [(j, i) for i, j in up]
        last = lax.slice_in_dim(array, length - width, length, axis=dim)
        initial = lax.slice_in_dim(array, 0, width, axis=dim)
        slabs[dim] = (lax.ppermute(last, axis, up), lax.ppermute(initial, axis, down))
    for position, (axis, dim) in enumerate(sides):
        before, after = slabs[dim]
        for _, other in sides[:position]:
            pad = [(0, 0)] * array.ndim
            pad[other] = (width, width)
            before = jnp.pad(before, pad)
            after = jnp.pad(after, pad)
        array = jnp.concatenate([before, array, after], axis=dim)
    return array


def for_sending(array):

    def short(part):
        return part.astype(jnp.bfloat16) if part.dtype == jnp.float32 else part

    return jax.tree.map(short, array)


def all_sum(values):
    axes = ("px", "py")
    count = lax.axis_size(axes)
    spread = jnp.broadcast_to(values[None], (count,) + values.shape)
    return jnp.sum(lax.all_to_all(spread, axes, 0, 0, tiled=True), 0)


def face_sum(padded, coeff_pad):
    values = padded[:, 1:-1, 1:-1]
    coeff = coeff_pad[:, 1:-1, 1:-1]
    height = values.shape[1]
    width = values.shape[2]
    result = jnp.zeros_like(values)
    for shift_y, shift_x in ((0, 1), (2, 1), (1, 0), (1, 2)):
        neighbour = padded[:, shift_y : shift_y + height, shift_x : shift_x + width]
        other = coeff_pad[:, shift_y : shift_y + height, shift_x : shift_x + width]
        result = result + 0.5 * (coeff + other) * (values - neighbour)
    vertical = 0.5 * (coeff[:-1] + coeff[1:]) * (values[:-1] - values[1:])
    zero_layer = jnp.zeros_like(values[:1])
    result = (
        result
        + jnp.concatenate((vertical, zero_layer), 0)
        - jnp.concatenate((zero_layer, vertical), 0)
    )
    return result


def exchange(block, axis, split_axis, concat_axis):
    size = lax.axis_size(axis)
    me = lax.axis_index(axis)
    piece = block.shape[split_axis] // size
    width = block.shape[concat_axis]
    shape = list(block.shape)
    shape[split_axis] = piece
    shape[concat_axis] = width * size
    result = jnp.zeros(shape, block.dtype)
    for shift in range(size):
        part = lax.dynamic_slice_in_dim(block, ((me + shift) % size) * piece, piece, split_axis)
        if shift:
            part = lax.ppermute(part, axis, [(i, (i + shift) % size) for i in range(size)])
        result = lax.dynamic_update_slice_in_dim(
            result, part, ((me - shift) % size) * width, concat_axis
        )
    return result


def precondition_lines(lines, first_level, eigenvectors, eigenvalues, level_shift):
    across = lax.axis_size("py")
    levels_here, rows, width = lines.shape
    cols = width // across
    first = jnp.dot(
        lines.reshape(levels_here * rows, width), eigenvectors, preferred_element_type=jnp.float32
    ).astype(jnp.bfloat16)
    outgoing = first.reshape(levels_here * rows, across, cols).transpose(1, 0, 2)
    incoming = lax.all_to_all(outgoing, "py", 0, 0, tiled=True)
    spectral = incoming.reshape(across, levels_here, rows, cols).transpose(1, 0, 2, 3)
    spectral = spectral.reshape(levels_here, across * rows, cols)
    second = jnp.einsum("jy,kyi->kji", eigenvectors, spectral, preferred_element_type=jnp.float32)
    eigen_cols = lax.dynamic_slice_in_dim(eigenvalues, lax.axis_index("py") * cols, cols, 0)
    shift_here = lax.dynamic_slice_in_dim(
        level_shift, first_level + lax.axis_index("px") * levels_here, levels_here, 0
    )
    denom = eigenvalues[None, :, None] + eigen_cols[None, None, :] + shift_here[:, None, None]
    scaled = (second / denom).astype(jnp.bfloat16)
    fourth = jnp.einsum(
        "yj,kji->kyi", eigenvectors, scaled, preferred_element_type=jnp.float32
    ).astype(jnp.bfloat16)
    edged = jnp.pad(fourth, ((0, 0), (1, 1), (0, 0)))
    outgoing = jnp.stack(
        [edged[:, target * rows : target * rows + rows + 2] for target in range(across)], 0
    )
    returned = lax.all_to_all(outgoing, "py", 0, 0, tiled=True)
    pencil = jnp.einsum(
        "qkyi,qix->kyx",
        returned,
        eigenvectors.reshape(across, cols, width),
        preferred_element_type=jnp.float32,
    )
    return return_lines(pencil.astype(jnp.bfloat16))


def precondition(residual, eigenvectors, eigenvalues, level_shift):
    levels = residual.shape[0]
    chunk = lax.axis_size("px")
    if levels % chunk or levels == chunk:
        chunk = levels
    parts = []
    waiting = residual
    for start in range(0, levels, chunk):
        lines = exchange(waiting[start : start + chunk].astype(jnp.bfloat16), "px", 0, 2)
        lines, waiting = lax.optimization_barrier((lines, waiting))
        parts.append(precondition_lines(lines, start, eigenvectors, eigenvalues, level_shift))
    return jnp.concatenate(parts, 0)


def return_lines(pencil):
    size = lax.axis_size("px")
    me = lax.axis_index("px")
    levels_here, rows, width = pencil.shape
    piece = width // size
    padded = jnp.pad(pencil, ((0, 0), (0, 0), (1, 1)))
    result = jnp.zeros((levels_here * size, rows, piece + 2), pencil.dtype)
    for shift in range(size):
        part = lax.dynamic_slice_in_dim(padded, ((me + shift) % size) * piece, piece + 2, 2)
        if shift:
            part = lax.ppermute(part, "px", [(i, (i + shift) % size) for i in range(size)])
        result = lax.dynamic_update_slice_in_dim(
            result, part, ((me - shift) % size) * levels_here, 0
        )
    return result


def operator(wide, coeff_pad):
    return face_sum(wide.astype(jnp.float32), coeff_pad)


def shards(right_side, solution_in, classes, coeff_table, eigenvectors, eigenvalues, level_shift):
    table = coeff_table.astype(jnp.bfloat16)
    choices = [table[label] for label in range(coeff_table.shape[0])]
    bit = 0
    while len(choices) > 1:
        chosen = (classes & (1 << bit)) != 0
        pairs = zip(choices[0::2], choices[1::2])
        choices = [jnp.where(chosen, high, low) for low, high in pairs]
        bit += 1
    coeff = jnp.broadcast_to(choices[0], classes.shape)
    stacked = padded_2(
        jnp.stack((solution_in, coeff)).astype(jnp.bfloat16), (("px", 3), ("py", 2)), 1
    )
    coeff_pad = stacked[1].astype(jnp.float32)
    solution = solution_in
    residual = right_side - face_sum(stacked[0].astype(jnp.float32), coeff_pad)
    direction = image = None
    gamma_prev = curvature_prev = None
    for iteration in range(ITERS):
        wide = precondition(residual, eigenvectors, eigenvalues, level_shift)
        precond = wide[:, 1:-1, 1:-1].astype(jnp.float32)
        precond_image = operator(wide, coeff_pad)
        if iteration == 0:
            sums = all_sum(jnp.stack((jnp.sum(residual * precond), jnp.sum(precond * precond_image))))
            gamma, curvature = sums[0], sums[1]
            direction, image = precond, precond_image
        else:
            sums = all_sum(
                jnp.stack(
                    (
                        jnp.sum(residual * precond),
                        jnp.sum(precond * precond_image),
                        jnp.sum(precond * image),
                        jnp.sum(direction * precond_image),
                    )
                )
            )
            gamma = sums[0]
            beta = gamma / gamma_prev
            curvature = sums[1] + beta * (sums[2] + sums[3]) + beta * beta * curvature_prev
            direction = precond + beta * direction
            image = precond_image + beta * image
        alpha = gamma / curvature
        solution = solution + alpha * direction
        residual = residual - alpha * image
        gamma_prev, curvature_prev = gamma, curvature
    return (solution, residual, direction)


def solution(mesh):
    in_specs = (P(None, "py", "px"), P(None, "py", "px"), P(None, "py", "px"), P(), P(), P(), P())
    out_specs = (P(None, "py", "px"), P(None, "py", "px"), P(None, "py", "px"))
    return jax.shard_map(shards, mesh=mesh, in_specs=in_specs, out_specs=out_specs, check_vma=False)
```
